128 devices in a mesh: stripe: 8 (over x_lo, y), frame: 16 (over z, x_hi, core).
Axes of the slice: x: 4 (x_hi: 2, x_lo: 2; x = x_hi * 2 + x_lo), y: 4, z: 4, core: 2. Of those that a mesh axis runs over, the one named last changes fastest.
Arguments:
- reference_img: bfloat16 [16384, 2048], P(('stripe', 'frame')), may hold values from -6 to 6
- frames: bfloat16 [256, 128, 2048], P(('stripe', 'frame')), may hold values from -6 to 6
- shifts: int32 [256], P(('stripe', 'frame')), may hold values from 0 to 2047
- dest_device: int32 [32768, 1], P(('stripe', 'frame')), may hold values from 0 to 127; in each aligned block of 256 rows (0 to 255, 256 to 511, ...) at most 4 rows name the same one
- dest_row: int32 [32768], P(('stripe', 'frame')), may hold values from 0 to 127
- visit_order: int32 [4], replicated, may hold values from 0 to 7, as said below
Outputs:
- correlation: float32 [256, 4, 2048], P(('stripe', 'frame'))
- blended: float32 [16384, 2048], P(('stripe', 'frame'))
The draws below stay inside these ranges and needn't reach their ends.
Inputs may be any that keep to these rules, and one draw needn't show every extreme that they name: `visit_order`: the 4 entries are distinct stripes. `dest_device`: the rows of one device name no band more than 4 times.
All inputs are finite; a program needn't handle non-finite values.
Results may differ from the reference program's by a relative error of at most 0.0057.
Values may be sent and summed in bfloat16 or wider, within the bound.
No kernel may reach another device: no remote copies, remote signals or barrier semaphores. Data moves between devices by JAX's collectives and lax.ppermute only.
A program may use at most 128 MiB of HBM per device.

```python
import math
import jax
import jax.numpy as jnp
import numpy as np
from jax import lax

W = 2048
BAND = 128
FD = 2
STEPS = 4
CAP = 4
NFRAMES = 256
ROWS = 16384
FRAME_ROWS = 32768
N_STRIPE = 8
N_FRAME = 16
DEVICES = 128


def draw_visit_order(key, part):
    return jax.random.permutation(key, N_STRIPE)[:STEPS].astype(jnp.int32)


def with_ends(values, own_key, smallest, largest):
    longest = values.shape.index(max(values.shape))
    spots = []
    for shift in (0, 1):
        where = [jax.random.randint(jax.random.fold_in(own_key, axis), (), 0, length) for axis, length in enumerate(values.shape)]
        where[longest] = (where[longest] + shift) % values.shape[longest]
        spots.append(tuple(where))
    return values.at[spots[0]].set(smallest).at[spots[1]].set(largest)


def shard_levels(own_key, dims, split, low, high):
    def one(position, parts):
        heights = jax.random.uniform(jax.random.fold_in(jax.random.fold_in(own_key, 6), position), (parts,), jnp.float32, low / len(split), high / len(split))
        return jnp.repeat(jnp.exp(heights), dims[position] // parts).reshape((-1,) + (1,) * (len(dims) - position - 1))

    gain = one(*split[0])
    for cut in split[1:]:
        gain = gain * one(*cut)
    return gain


def deal_out(key, own, number, rows, count, top, bound, lean):
    ranking = jax.random.permutation(key, count)
    heavy_load, ordinary = load_shares(count, rows * top, bound, lean, True), load_shares(count, rows * top, bound, lean, False)
    places = jnp.arange(count)

    def named(sizes, rotation):
        used = int((sizes > 0).sum())
        fixed = max(1, used // 4)
        shifted = fixed + (places - fixed + rotation * (used - fixed)) % max(1, count - fixed)
        return jnp.zeros((count,), jnp.int32).at[ranking[jnp.where(places < fixed, places, shifted)]].set(jnp.asarray(sizes, jnp.int32))

    sizes = jnp.where(number % 4 == 0, named(heavy_load, number // 4), named(ordinary, number - number // 4 - 1))
    mixed = jax.random.permutation(jax.random.fold_in(own, 3), count)
    donor, taker = mixed[0:count // 2 * 2:2], mixed[1:count // 2 * 2:2]
    margin = jnp.minimum(sizes[donor] - 1, bound - sizes[taker]) // 2
    margin = jnp.where((donor == ranking[0]) | (taker == ranking[0]) | (sizes[taker] == 0), 0, jnp.maximum(margin, 0))
    shifted = jax.random.randint(jax.random.fold_in(own, 4), (count // 2,), 0, 1 << 20) % (margin + 1)
    sizes = sizes.at[donor].add(-shifted).at[taker].add(shifted)
    items = jnp.searchsorted(jnp.cumsum(sizes), jnp.arange(rows * top), side="right").astype(jnp.int32)
    grid = items.reshape(top, rows).T
    grid = grid[jax.random.permutation(jax.random.fold_in(own, 1), rows)]
    rotation = jax.random.randint(jax.random.fold_in(own, 2), (rows, 1), 0, top)
    return jnp.take_along_axis(grid, (jnp.arange(top)[None, :] + rotation) % top, axis=1)


def load_shares(count, total, reach, skew, full):
    portions = [(1 << 20) // math.isqrt(rank ** skew) + 1 for rank in range(1, count + 1)]
    largest = reach if full else min(reach, max(-(-total // count), total * portions[0] // sum(portions)))
    least = 1 if total - largest >= count - 1 else 0
    holding, rest = [largest] + [least] * (count - 1), total - largest - least * (count - 1)
    while rest > 0:
        movable = [i for i in range(1, count) if holding[i] < largest] or [i for i in range(1, count) if holding[i] < reach]
        whole, remaining = sum([portions[i] for i in movable]), rest
        for i in movable:
            more = min(reach - holding[i], max(1, remaining * portions[i] // whole), rest)
            holding[i] = holding[i] + more
            rest = rest - more
    return np.array(holding)


def gaussian(rng, shape, width, bound, pieces=(), kind=jnp.bfloat16):
    factor_of = shard_levels(rng, shape, pieces, -0.22, 0.18) if pieces else 1.0
    entries = jax.random.normal(rng, shape, jnp.float32) * width * factor_of
    return jnp.minimum(jnp.maximum(entries, -bound), bound).astype(kind)


def setup_inputs(seed: int = 0) -> dict:
    seeds = jax.random.split(jax.random.key(seed), 7)
    reference_img = gaussian(seeds[0], (ROWS, W), 1.0, 6.0, ((0, 128),))
    frames = gaussian(seeds[1], (NFRAMES, BAND, W), 1.0, 6.0, ((0, 128),))
    shifts = with_ends(jax.random.randint(seeds[2], (NFRAMES,), 0, W), jax.random.fold_in(seeds[2], 1), 0, W - 1).astype(jnp.int32)
    dest_device_keys = jax.random.split(jax.random.fold_in(seeds[3], 1), FRAME_ROWS // (FD * BAND))
    dest_device_turns = jax.random.permutation(jax.random.fold_in(seeds[3], 3), FRAME_ROWS // (FD * BAND))
    dest_device = jax.vmap(lambda own, number: deal_out(jax.random.fold_in(seeds[3], 2), own, number, FD * BAND, DEVICES, 1, CAP, 2))(dest_device_keys, dest_device_turns).reshape((FRAME_ROWS, 1))
    dest_row = with_ends(jax.random.randint(seeds[4], (FRAME_ROWS,), 0, BAND), jax.random.fold_in(seeds[4], 1), 0, BAND - 1).astype(jnp.int32)
    visit_order = draw_visit_order(jax.random.fold_in(seeds[6], 71), 0)
    return dict(reference_img=reference_img, frames=frames, shifts=shifts, dest_device=dest_device, dest_row=dest_row, visit_order=visit_order)


def basis_table(pixels):
    indices = jnp.arange(pixels, dtype=jnp.int32)
    products = indices[:, None] * indices[None, :] % pixels
    phases = products.astype(jnp.float32) * (2.0 * math.pi / pixels)
    return jnp.concatenate([jnp.cos(phases), -jnp.sin(phases)], axis=1).astype(jnp.bfloat16)

def correlate(frame_block, band_specs, dft_basis, band_rows):
    pixels = frame_block.shape[-1]
    count_frames = frame_block.shape[0]
    spectra = jnp.dot(frame_block.reshape(count_frames * band_rows, pixels), dft_basis, preferred_element_type=jnp.float32)
    spectra = spectra.reshape(count_frames, band_rows, 2 * pixels)
    spec_re = spectra[:, :, :pixels]
    spec_im = spectra[:, :, pixels:]
    frame_power = lax.optimization_barrier(jnp.sum(spec_re * spec_re + spec_im * spec_im, axis=1))
    results = []
    for step in range(band_specs.shape[0]):
        band_f = band_specs[step].astype(jnp.float32)
        band_re = band_f[:, :pixels]
        band_im = band_f[:, pixels:]
        band_power = lax.optimization_barrier(jnp.sum(band_re * band_re + band_im * band_im, axis=0))
        high = lax.Precision.HIGHEST
        cross_re = jnp.einsum('fiu,iu->fu', spec_re, band_re, precision=high) + jnp.einsum('fiu,iu->fu', spec_im, band_im, precision=high)
        cross_im = jnp.einsum('fiu,iu->fu', spec_im, band_re, precision=high) - jnp.einsum('fiu,iu->fu', spec_re, band_im, precision=high)
        magnitude = jnp.sqrt(frame_power * band_power[None, :] + 1e-06)
        coherence = jnp.concatenate([cross_re / magnitude, cross_im / magnitude], axis=1).astype(jnp.bfloat16)
        surface = lax.dot_general(coherence, dft_basis, (((1,), (1,)), ((), ())), preferred_element_type=jnp.float32)
        results.append(surface * math.sqrt(band_rows / pixels))
    return jnp.stack(results, axis=1)

def reference(reference_img, frames, shifts, dest_device, dest_row, visit_order):
    dft_basis = basis_table(W)
    stripe_rows = N_FRAME * BAND

    def stripe_spectrum(root_idx):
        ref_rows = lax.dynamic_slice_in_dim(reference_img, (root_idx * stripe_rows).astype(jnp.int32), stripe_rows, 0)
        spectra = jnp.dot(ref_rows, dft_basis, preferred_element_type=jnp.float32).astype(jnp.bfloat16)
        return spectra.reshape(N_FRAME, BAND, 2 * W)
    band_spectra = jnp.stack([stripe_spectrum(visit_order[step]) for step in range(STEPS)])

    def one_block(device_id):
        frame_block = lax.dynamic_slice_in_dim(frames, (device_id * FD).astype(jnp.int32), FD, 0)
        band_specs = lax.dynamic_index_in_dim(band_spectra, (device_id % N_FRAME).astype(jnp.int32), 1, keepdims=False)
        return correlate(frame_block, band_specs, dft_basis, BAND)
    correlation = lax.map(one_block, jnp.arange(DEVICES, dtype=jnp.int32)).reshape(NFRAMES, STEPS, W)
    placed = jax.vmap(lambda frame_img, amount: jnp.roll(frame_img, amount, axis=1))(frames, shifts)
    placed = placed.reshape(FRAME_ROWS, W).astype(jnp.float32)
    target = (dest_device[:, 0] * BAND + dest_row).astype(jnp.int32)
    landed = jax.ops.segment_sum(placed, target, num_segments=ROWS)
    land_count = jax.ops.segment_sum(jnp.ones((FRAME_ROWS,), jnp.float32), target, num_segments=ROWS)
    blended = (reference_img.astype(jnp.float32) + landed) / (1.0 + land_count[:, None])
    return (correlation, blended)
```

```python
import math

import jax
import jax.numpy as jnp
from jax import lax
from jax.sharding import PartitionSpec as P


def basis_halves(pixels):
    lo_count = 64 if pixels % 64 == 0 else 1
    hi_count = pixels // lo_count
    u = jnp.arange(pixels, dtype=jnp.int32)
    scale = 2.0 * math.pi / pixels
    hi = jnp.arange(hi_count, dtype=jnp.int32)
    lo = jnp.arange(lo_count, dtype=jnp.int32)
    phase_hi = (hi[:, None] * lo_count * u[None, :] % pixels).astype(jnp.float32) * scale
    phase_lo = (lo[:, None] * u[None, :] % pixels).astype(jnp.float32) * scale
    c1, s1 = jnp.cos(phase_hi)[:, None, :], jnp.sin(phase_hi)[:, None, :]
    c2, s2 = jnp.cos(phase_lo)[None, :, :], jnp.sin(phase_lo)[None, :, :]
    cos_t = (c1 * c2 - s1 * s2).reshape(pixels, pixels).astype(jnp.bfloat16)
    nsin_t = (-(s1 * c2 + c1 * s2)).reshape(pixels, pixels).astype(jnp.bfloat16)
    return cos_t, nsin_t


def shift_rows(frame_img, amount):
    pixels = frame_img.shape[-1]
    doubled = jnp.concatenate([frame_img, frame_img], axis=1)
    start = pixels - lax.rem(amount, pixels)
    return lax.dynamic_slice_in_dim(doubled, start, pixels, axis=1)


def per_device(reference_img, frames, shifts, dest_device, dest_row, visit_order):
    count_frames, band_rows, pixels = frames.shape
    cos_t, nsin_t = basis_halves(pixels)
    steps = visit_order.shape[0]

    gathered = lax.all_gather(reference_img, "stripe")
    visited = jnp.take(gathered, visit_order, axis=0, mode="clip")

    frame_flat = frames.reshape(count_frames * band_rows, pixels)
    spec_re = jnp.dot(frame_flat, cos_t, preferred_element_type=jnp.float32).reshape(
        count_frames, band_rows, pixels
    )
    spec_im = jnp.dot(frame_flat, nsin_t, preferred_element_type=jnp.float32).reshape(
        count_frames, band_rows, pixels
    )
    frame_power = jnp.sum(spec_re * spec_re + spec_im * spec_im, axis=1)

    visited_flat = visited.reshape(steps * band_rows, pixels)
    band_re = (
        jnp.dot(visited_flat, cos_t, preferred_element_type=jnp.float32)
        .astype(jnp.bfloat16)
        .astype(jnp.float32)
        .reshape(steps, band_rows, pixels)
    )
    band_im = (
        jnp.dot(visited_flat, nsin_t, preferred_element_type=jnp.float32)
        .astype(jnp.bfloat16)
        .astype(jnp.float32)
        .reshape(steps, band_rows, pixels)
    )
    band_power = jnp.sum(band_re * band_re + band_im * band_im, axis=1)

    fr = spec_re[:, None]
    fi = spec_im[:, None]
    br = band_re[None]
    bi = band_im[None]
    cross_re = jnp.sum(fr * br, axis=2) + jnp.sum(fi * bi, axis=2)
    cross_im = jnp.sum(fi * br, axis=2) - jnp.sum(fr * bi, axis=2)
    magnitude = jnp.sqrt(frame_power[:, None, :] * band_power[None, :, :] + 1e-06)
    coh_re = (cross_re / magnitude).astype(jnp.bfloat16).reshape(count_frames * steps, pixels)
    coh_im = (cross_im / magnitude).astype(jnp.bfloat16).reshape(count_frames * steps, pixels)
    surface = jnp.dot(coh_re, cos_t, preferred_element_type=jnp.float32) + jnp.dot(
        coh_im, nsin_t, preferred_element_type=jnp.float32
    )
    correlation = (surface * math.sqrt(band_rows / pixels)).reshape(count_frames, steps, pixels)

    num_devices = lax.axis_size("stripe") * lax.axis_size("frame")
    frame_rows = count_frames * band_rows
    capacity = max(2, 2 * frame_rows // num_devices)
    placed = jnp.concatenate(
        [shift_rows(frames[f], shifts[f]) for f in range(count_frames)], axis=0
    )
    target_dev = dest_device[:, 0]
    onehot = (target_dev[:, None] == jnp.arange(num_devices, dtype=jnp.int32)[None, :]).astype(
        jnp.int32
    )
    row_rank = jnp.sum((jnp.cumsum(onehot, axis=0) - 1) * onehot, axis=1)
    slot_id = target_dev * capacity + row_rank
    select = slot_id[None, :] == jnp.arange(num_devices * capacity, dtype=jnp.int32)[:, None]
    outgoing = jnp.dot(
        select.astype(jnp.bfloat16), placed, preferred_element_type=jnp.float32
    ).astype(jnp.bfloat16)
    filled = jnp.any(select, axis=1)
    local_row = jnp.sum(jnp.where(select, dest_row[None, :], 0), axis=1)
    out_index = jnp.where(filled, local_row, -1).astype(jnp.float32).astype(jnp.bfloat16)
    lanes = 128
    index_block = jnp.pad(
        out_index.reshape(num_devices, capacity), ((0, 0), (0, lanes - capacity)), constant_values=-1
    )
    packed = jnp.concatenate(
        [outgoing.reshape(num_devices, capacity * pixels), index_block], axis=1
    )
    received = lax.all_to_all(packed, ("stripe", "frame"), split_axis=0, concat_axis=0, tiled=True)
    incoming = received[:, : capacity * pixels].reshape(num_devices * capacity, pixels)
    index_f = received[:, capacity * pixels : capacity * pixels + capacity].reshape(-1).astype(
        jnp.float32
    )
    hits = index_f[None, :] == jnp.arange(band_rows, dtype=jnp.float32)[:, None]
    landed = jnp.dot(hits.astype(jnp.bfloat16), incoming, preferred_element_type=jnp.float32)
    land_count = jnp.sum(hits.astype(jnp.float32), axis=1)
    blended = (reference_img.astype(jnp.float32) + landed) / (1.0 + land_count[:, None])
    return (correlation, blended)


def solution(mesh):
    placed = (
        P(("stripe", "frame"), None),
        P(("stripe", "frame"), None, None),
        P(("stripe", "frame")),
        P(("stripe", "frame"), None),
        P(("stripe", "frame")),
        P(),
    )
    return jax.shard_map(
        per_device,
        mesh=mesh,
        in_specs=placed,
        out_specs=(P(("stripe", "frame"), None, None), P(("stripe", "frame"), None)),
        check_vma=False,
    )
```

```python
import math

import jax
import jax.numpy as jnp
from jax import lax
from jax.sharding import PartitionSpec as P


def basis_halves(pixels, columns):
    lo_count = 64 if pixels % 64 == 0 else 1
    hi_count = pixels // lo_count
    u = jnp.arange(columns, dtype=jnp.int32)
    scale = 2.0 * math.pi / pixels
    hi = jnp.arange(hi_count, dtype=jnp.int32)
    lo = jnp.arange(lo_count, dtype=jnp.int32)
    phase_hi = (hi[:, None] * lo_count * u[None, :] % pixels).astype(jnp.float32) * scale
    phase_lo = (lo[:, None] * u[None, :] % pixels).astype(jnp.float32) * scale
    c1, s1 = jnp.cos(phase_hi)[:, None, :], jnp.sin(phase_hi)[:, None, :]
    c2, s2 = jnp.cos(phase_lo)[None, :, :], jnp.sin(phase_lo)[None, :, :]
    cos_t = (c1 * c2 - s1 * s2).reshape(pixels, columns).astype(jnp.bfloat16)
    nsin_t = (-(s1 * c2 + c1 * s2)).reshape(pixels, columns).astype(jnp.bfloat16)
    return cos_t, nsin_t


def shift_rows(frame_img, amount):
    pixels = frame_img.shape[-1]
    doubled = jnp.concatenate([frame_img, frame_img], axis=1)
    start = pixels - lax.rem(amount, pixels)
    return lax.dynamic_slice_in_dim(doubled, start, pixels, axis=1)


def per_device(reference_img, frames, shifts, dest_device, dest_row, visit_order):
    count_frames, band_rows, pixels = frames.shape
    steps = visit_order.shape[0]
    half = pixels // 2
    columns = min(pixels, half + 128)
    cos_t, nsin_t = basis_halves(pixels, columns)
    col = jnp.arange(columns, dtype=jnp.int32)
    weight = jnp.where((col == 0) | (col == half), 1.0, jnp.where(col < half, 2.0, 0.0))

    gathered = lax.all_gather(reference_img, "stripe")
    visited = jnp.take(gathered, visit_order, axis=0, mode="clip")

    frame_flat = frames.reshape(count_frames * band_rows, pixels)
    spec_re = jnp.dot(frame_flat, cos_t, preferred_element_type=jnp.float32).reshape(
        count_frames, band_rows, columns
    )
    spec_im = jnp.dot(frame_flat, nsin_t, preferred_element_type=jnp.float32).reshape(
        count_frames, band_rows, columns
    )
    frame_power = jnp.sum(spec_re * spec_re + spec_im * spec_im, axis=1)

    visited_flat = visited.reshape(steps * band_rows, pixels)
    band_re = (
        jnp.dot(visited_flat, cos_t, preferred_element_type=jnp.float32)
        .astype(jnp.bfloat16)
        .astype(jnp.float32)
        .reshape(steps, band_rows, columns)
    )
    band_im = (
        jnp.dot(visited_flat, nsin_t, preferred_element_type=jnp.float32)
        .astype(jnp.bfloat16)
        .astype(jnp.float32)
        .reshape(steps, band_rows, columns)
    )
    band_power = jnp.sum(band_re * band_re + band_im * band_im, axis=1)

    fr = spec_re[:, None]
    fi = spec_im[:, None]
    br = band_re[None]
    bi = band_im[None]
    cross_re = jnp.sum(fr * br, axis=2) + jnp.sum(fi * bi, axis=2)
    cross_im = jnp.sum(fi * br, axis=2) - jnp.sum(fr * bi, axis=2)
    magnitude = jnp.sqrt(frame_power[:, None, :] * band_power[None, :, :] + 1e-06)
    coh_re = (cross_re / magnitude).astype(jnp.bfloat16).astype(jnp.float32) * weight
    coh_im = (cross_im / magnitude).astype(jnp.bfloat16).astype(jnp.float32) * weight
    coh_re = coh_re.astype(jnp.bfloat16).reshape(count_frames * steps, columns)
    coh_im = coh_im.astype(jnp.bfloat16).reshape(count_frames * steps, columns)
    contract = (((1,), (1,)), ((), ()))
    surface = lax.dot_general(
        coh_re, cos_t, contract, preferred_element_type=jnp.float32
    ) + lax.dot_general(coh_im, nsin_t, contract, preferred_element_type=jnp.float32)
    correlation = (surface * math.sqrt(band_rows / pixels)).reshape(count_frames, steps, pixels)

    num_devices = lax.axis_size("stripe") * lax.axis_size("frame")
    frame_rows = count_frames * band_rows
    capacity = max(2, 2 * frame_rows // num_devices)
    placed = jnp.concatenate(
        [shift_rows(frames[f], shifts[f]) for f in range(count_frames)], axis=0
    )
    target_dev = dest_device[:, 0]
    onehot = (target_dev[:, None] == jnp.arange(num_devices, dtype=jnp.int32)[None, :]).astype(
        jnp.int32
    )
    row_rank = jnp.sum((jnp.cumsum(onehot, axis=0) - 1) * onehot, axis=1)
    slot_id = target_dev * capacity + row_rank
    select = slot_id[None, :] == jnp.arange(num_devices * capacity, dtype=jnp.int32)[:, None]
    select3 = select.reshape(num_devices, capacity, frame_rows)
    outgoing = jnp.einsum(
        "dsr,rx->dsx", select3.astype(jnp.bfloat16), placed, preferred_element_type=jnp.float32
    ).astype(jnp.bfloat16)
    filled = jnp.any(select3, axis=2)
    local_row = jnp.sum(jnp.where(select3, dest_row[None, None, :], 0), axis=2)
    out_index = jnp.where(filled, local_row, -1).astype(jnp.float32).astype(jnp.bfloat16)
    lanes = 128
    index_cols = jnp.broadcast_to(out_index[:, :, None], (num_devices, capacity, lanes))
    packed = jnp.concatenate([outgoing, index_cols], axis=2)
    received = lax.all_to_all(packed, ("stripe", "frame"), split_axis=0, concat_axis=0, tiled=True)
    incoming = received[:, :, :pixels]
    index_f = received[:, :, pixels].astype(jnp.float32)
    hits = index_f[None, :, :] == jnp.arange(band_rows, dtype=jnp.float32)[:, None, None]
    landed = jnp.einsum(
        "tps,psx->tx", hits.astype(jnp.bfloat16), incoming, preferred_element_type=jnp.float32
    )
    land_count = jnp.sum(hits.astype(jnp.float32), axis=(1, 2))
    blended = (reference_img.astype(jnp.float32) + landed) / (1.0 + land_count[:, None])
    return (correlation, blended)


def solution(mesh):
    placed = (
        P(("stripe", "frame"), None),
        P(("stripe", "frame"), None, None),
        P(("stripe", "frame")),
        P(("stripe", "frame"), None),
        P(("stripe", "frame")),
        P(),
    )
    return jax.shard_map(
        per_device,
        mesh=mesh,
        in_specs=placed,
        out_specs=(P(("stripe", "frame"), None, None), P(("stripe", "frame"), None)),
        check_vma=False,
    )
```

```python
import math

import jax
import jax.numpy as jnp
from jax import lax
from jax.sharding import PartitionSpec as P


def dft_table(rows, columns, pixels):
    lo_count = 64 if rows % 64 == 0 else 1
    hi_count = rows // lo_count
    c = jnp.arange(columns, dtype=jnp.int32)
    scale = 2.0 * math.pi / pixels
    hi = jnp.arange(hi_count, dtype=jnp.int32)
    lo = jnp.arange(lo_count, dtype=jnp.int32)
    phase_hi = (hi[:, None] * lo_count * c[None, :] % pixels).astype(jnp.float32) * scale
    phase_lo = (lo[:, None] * c[None, :] % pixels).astype(jnp.float32) * scale
    c1, s1 = jnp.cos(phase_hi)[:, None, :], jnp.sin(phase_hi)[:, None, :]
    c2, s2 = jnp.cos(phase_lo)[None, :, :], jnp.sin(phase_lo)[None, :, :]
    cos_t = (c1 * c2 - s1 * s2).reshape(rows, columns)
    nsin_t = (-(s1 * c2 + c1 * s2)).reshape(rows, columns)
    return cos_t.astype(jnp.bfloat16), nsin_t.astype(jnp.bfloat16)


def shift_rows(frame_img, amount):
    pixels = frame_img.shape[-1]
    doubled = jnp.concatenate([frame_img, frame_img], axis=1)
    start = pixels - lax.rem(amount, pixels)
    return lax.dynamic_slice_in_dim(doubled, start, pixels, axis=1)


def per_device(reference_img, frames, shifts, dest_device, dest_row, visit_order):
    count_frames, band_rows, pixels = frames.shape
    steps = visit_order.shape[0]
    half = pixels // 2
    columns = min(pixels, half + 128)
    fwd_cos, fwd_sin = dft_table(pixels, columns, pixels)
    forward = jnp.concatenate([fwd_cos, fwd_sin], axis=1)
    inv_cos, inv_sin = dft_table(columns, pixels, pixels)
    inverse = jnp.concatenate([inv_cos, inv_sin], axis=0)
    col = jnp.arange(columns, dtype=jnp.int32)
    weight = jnp.where((col == 0) | (col == half), 1.0, jnp.where(col < half, 2.0, 0.0))

    pieces = 2 if band_rows % 32 == 0 else 1
    piece_rows = band_rows // pieces
    gathered = [
        lax.all_gather(reference_img[p * piece_rows : (p + 1) * piece_rows], "stripe")
        for p in range(pieces)
    ]

    frame_flat = frames.reshape(count_frames * band_rows, pixels)
    spectra = jnp.dot(frame_flat, forward, preferred_element_type=jnp.float32).reshape(
        count_frames, band_rows, 2 * columns
    )
    spec_re = spectra[:, :, :columns]
    spec_im = spectra[:, :, columns:]
    frame_power = jnp.sum(spec_re * spec_re + spec_im * spec_im, axis=1)

    band_power = 0.0
    cross_re = 0.0
    cross_im = 0.0
    for p in range(pieces):
        visited = jnp.take(gathered[p], visit_order, axis=0, mode="clip")
        band = (
            jnp.dot(
                visited.reshape(steps * piece_rows, pixels),
                forward,
                preferred_element_type=jnp.float32,
            )
            .astype(jnp.bfloat16)
            .astype(jnp.float32)
            .reshape(steps, piece_rows, 2 * columns)
        )
        band_re = band[:, :, :columns]
        band_im = band[:, :, columns:]
        band_power = band_power + jnp.sum(band_re * band_re + band_im * band_im, axis=1)
        fr = spec_re[:, None, p * piece_rows : (p + 1) * piece_rows]
        fi = spec_im[:, None, p * piece_rows : (p + 1) * piece_rows]
        br = band_re[None]
        bi = band_im[None]
        cross_re = cross_re + (jnp.sum(fr * br, axis=2) + jnp.sum(fi * bi, axis=2))
        cross_im = cross_im + (jnp.sum(fi * br, axis=2) - jnp.sum(fr * bi, axis=2))
    magnitude = jnp.sqrt(frame_power[:, None, :] * band_power[None, :, :] + 1e-06)
    coh_re = (cross_re / magnitude).astype(jnp.bfloat16).astype(jnp.float32) * weight
    coh_im = (cross_im / magnitude).astype(jnp.bfloat16).astype(jnp.float32) * weight
    coherence = jnp.concatenate([coh_re, coh_im], axis=2).astype(jnp.bfloat16)
    surface = jnp.dot(
        coherence.reshape(count_frames * steps, 2 * columns),
        inverse,
        preferred_element_type=jnp.float32,
    )
    correlation = (surface * math.sqrt(band_rows / pixels)).reshape(count_frames, steps, pixels)

    num_devices = lax.axis_size("stripe") * lax.axis_size("frame")
    frame_rows = count_frames * band_rows
    capacity = max(2, 2 * frame_rows // num_devices)
    placed = jnp.concatenate(
        [shift_rows(frames[f], shifts[f]) for f in range(count_frames)], axis=0
    )
    target_dev = dest_device[:, 0]
    onehot = (target_dev[:, None] == jnp.arange(num_devices, dtype=jnp.int32)[None, :]).astype(
        jnp.int32
    )
    row_rank = jnp.sum((jnp.cumsum(onehot, axis=0) - 1) * onehot, axis=1)
    slot_id = target_dev * capacity + row_rank
    select = slot_id[None, :] == jnp.arange(num_devices * capacity, dtype=jnp.int32)[:, None]
    select3 = select.reshape(num_devices, capacity, frame_rows)
    outgoing = jnp.einsum(
        "dsr,rx->dsx", select3.astype(jnp.bfloat16), placed, preferred_element_type=jnp.float32
    ).astype(jnp.bfloat16)
    filled = jnp.any(select3, axis=2)
    local_row = jnp.sum(jnp.where(select3, dest_row[None, None, :], 0), axis=2)
    out_index = jnp.where(filled, local_row, -1).astype(jnp.float32).astype(jnp.bfloat16)
    lanes = 128
    index_cols = jnp.broadcast_to(out_index[:, :, None], (num_devices, capacity, lanes))
    packed = jnp.concatenate([outgoing, index_cols], axis=2)
    received = lax.all_to_all(packed, ("stripe", "frame"), split_axis=0, concat_axis=0, tiled=True)
    incoming = received[:, :, :pixels]
    index_f = received[:, :, pixels].astype(jnp.float32)
    hits = index_f[None, :, :] == jnp.arange(band_rows, dtype=jnp.float32)[:, None, None]
    landed = jnp.einsum(
        "tps,psx->tx", hits.astype(jnp.bfloat16), incoming, preferred_element_type=jnp.float32
    )
    land_count = jnp.sum(hits.astype(jnp.float32), axis=(1, 2))
    blended = (reference_img.astype(jnp.float32) + landed) / (1.0 + land_count[:, None])
    return (correlation, blended)


def solution(mesh):
    placed = (
        P(("stripe", "frame"), None),
        P(("stripe", "frame"), None, None),
        P(("stripe", "frame")),
        P(("stripe", "frame"), None),
        P(("stripe", "frame")),
        P(),
    )
    return jax.shard_map(
        per_device,
        mesh=mesh,
        in_specs=placed,
        out_specs=(P(("stripe", "frame"), None, None), P(("stripe", "frame"), None)),
        check_vma=False,
    )
```

```python
import math

import jax
import jax.numpy as jnp
from jax import lax
from jax.sharding import PartitionSpec as P


def dft_table(rows, columns, pixels):
    lo_count = 64 if rows % 64 == 0 else 1
    hi_count = rows // lo_count
    c = jnp.arange(columns, dtype=jnp.int32)
    scale = 2.0 * math.pi / pixels
    hi = jnp.arange(hi_count, dtype=jnp.int32)
    lo = jnp.arange(lo_count, dtype=jnp.int32)
    phase_hi = (hi[:, None] * lo_count * c[None, :] % pixels).astype(jnp.float32) * scale
    phase_lo = (lo[:, None] * c[None, :] % pixels).astype(jnp.float32) * scale
    c1, s1 = jnp.cos(phase_hi)[:, None, :], jnp.sin(phase_hi)[:, None, :]
    c2, s2 = jnp.cos(phase_lo)[None, :, :], jnp.sin(phase_lo)[None, :, :]
    cos_t = (c1 * c2 - s1 * s2).reshape(rows, columns)
    nsin_t = (-(s1 * c2 + c1 * s2)).reshape(rows, columns)
    return cos_t.astype(jnp.bfloat16), nsin_t.astype(jnp.bfloat16)


def shift_rows(frame_img, amount):
    pixels = frame_img.shape[-1]
    doubled = jnp.concatenate([frame_img, frame_img], axis=1)
    start = pixels - lax.rem(amount, pixels)
    return lax.dynamic_slice_in_dim(doubled, start, pixels, axis=1)


def per_device(reference_img, frames, shifts, dest_device, dest_row, visit_order):
    count_frames, band_rows, pixels = frames.shape
    steps = visit_order.shape[0]
    stripes = lax.axis_size("stripe")
    half = pixels // 2
    columns = min(pixels, half + 128)
    fwd_cos, fwd_sin = dft_table(pixels, columns, pixels)
    forward = jnp.concatenate([fwd_cos, fwd_sin], axis=1)
    inv_cos, inv_sin = dft_table(columns, pixels, pixels)
    inverse = jnp.concatenate([inv_cos, inv_sin], axis=0)
    col = jnp.arange(columns, dtype=jnp.int32)
    weight = jnp.where((col == 0) | (col == half), 1.0, jnp.where(col < half, 2.0, 0.0))

    chunk = band_rows // stripes
    frame_part = frames.reshape(count_frames, stripes, chunk, pixels).transpose(1, 0, 2, 3)
    frame_part = frame_part.reshape(stripes, count_frames * chunk, pixels)
    band_part = reference_img.reshape(stripes, chunk, pixels)
    outbound = jnp.concatenate([frame_part, band_part], axis=1)
    inbound = lax.all_to_all(outbound, "stripe", split_axis=0, concat_axis=0, tiled=True)
    frame_rows_in = inbound[:, : count_frames * chunk].reshape(stripes * count_frames * chunk, pixels)
    band_in = inbound[:, count_frames * chunk :]
    visited = jnp.take(band_in, visit_order, axis=0, mode="clip").reshape(steps * chunk, pixels)

    spectra = jnp.dot(frame_rows_in, forward, preferred_element_type=jnp.float32).reshape(
        stripes, count_frames, 1, chunk, 2 * columns
    )
    spec_re = spectra[..., :columns]
    spec_im = spectra[..., columns:]
    band = (
        jnp.dot(visited, forward, preferred_element_type=jnp.float32)
        .astype(jnp.bfloat16)
        .astype(jnp.float32)
        .reshape(steps, chunk, 2 * columns)
    )
    band_re = band[..., :columns]
    band_im = band[..., columns:]
    frame_power = jnp.sum(spec_re * spec_re + spec_im * spec_im, axis=3)[:, :, 0]
    band_power = jnp.sum(band_re * band_re + band_im * band_im, axis=1)
    br = band_re[None, None]
    bi = band_im[None, None]
    cross_re = jnp.sum(spec_re * br, axis=3) + jnp.sum(spec_im * bi, axis=3)
    cross_im = jnp.sum(spec_im * br, axis=3) - jnp.sum(spec_re * bi, axis=3)
    partial = jnp.concatenate(
        [
            cross_re.reshape(stripes, count_frames * steps, columns),
            cross_im.reshape(stripes, count_frames * steps, columns),
            frame_power,
            jnp.broadcast_to(band_power[None], (stripes, steps, columns)),
        ],
        axis=1,
    )
    total = jnp.sum(
        lax.all_to_all(partial, "stripe", split_axis=0, concat_axis=0, tiled=True), axis=0
    )
    pairs = count_frames * steps
    cross_re = total[:pairs].reshape(count_frames, steps, columns)
    cross_im = total[pairs : 2 * pairs].reshape(count_frames, steps, columns)
    frame_power = total[2 * pairs : 2 * pairs + count_frames]
    band_power = total[2 * pairs + count_frames :]

    magnitude = jnp.sqrt(frame_power[:, None, :] * band_power[None, :, :] + 1e-06)
    coh_re = (cross_re / magnitude).astype(jnp.bfloat16).astype(jnp.float32) * weight
    coh_im = (cross_im / magnitude).astype(jnp.bfloat16).astype(jnp.float32) * weight
    coherence = jnp.concatenate([coh_re, coh_im], axis=2).astype(jnp.bfloat16)
    surface = jnp.dot(
        coherence.reshape(count_frames * steps, 2 * columns),
        inverse,
        preferred_element_type=jnp.float32,
    )
    correlation = (surface * math.sqrt(band_rows / pixels)).reshape(count_frames, steps, pixels)

    num_devices = lax.axis_size("stripe") * lax.axis_size("frame")
    frame_rows = count_frames * band_rows
    capacity = max(2, 2 * frame_rows // num_devices)
    placed = jnp.concatenate(
        [shift_rows(frames[f], shifts[f]) for f in range(count_frames)], axis=0
    )
    target_dev = dest_device[:, 0]
    onehot = (target_dev[:, None] == jnp.arange(num_devices, dtype=jnp.int32)[None, :]).astype(
        jnp.int32
    )
    row_rank = jnp.sum((jnp.cumsum(onehot, axis=0) - 1) * onehot, axis=1)
    slot_id = target_dev * capacity + row_rank
    select = slot_id[None, :] == jnp.arange(num_devices * capacity, dtype=jnp.int32)[:, None]
    select3 = select.reshape(num_devices, capacity, frame_rows)
    outgoing = jnp.einsum(
        "dsr,rx->dsx", select3.astype(jnp.bfloat16), placed, preferred_element_type=jnp.float32
    ).astype(jnp.bfloat16)
    filled = jnp.any(select3, axis=2)
    local_row = jnp.sum(jnp.where(select3, dest_row[None, None, :], 0), axis=2)
    out_index = jnp.where(filled, local_row, -1).astype(jnp.float32).astype(jnp.bfloat16)
    lanes = 128
    index_cols = jnp.broadcast_to(out_index[:, :, None], (num_devices, capacity, lanes))
    packed = jnp.concatenate([outgoing, index_cols], axis=2)
    received = lax.all_to_all(packed, ("stripe", "frame"), split_axis=0, concat_axis=0, tiled=True)
    incoming = received[:, :, :pixels]
    index_f = received[:, :, pixels].astype(jnp.float32)
    hits = index_f[None, :, :] == jnp.arange(band_rows, dtype=jnp.float32)[:, None, None]
    landed = jnp.einsum(
        "tps,psx->tx", hits.astype(jnp.bfloat16), incoming, preferred_element_type=jnp.float32
    )
    land_count = jnp.sum(hits.astype(jnp.float32), axis=(1, 2))
    blended = (reference_img.astype(jnp.float32) + landed) / (1.0 + land_count[:, None])
    return (correlation, blended)


def solution(mesh):
    placed = (
        P(("stripe", "frame"), None),
        P(("stripe", "frame"), None, None),
        P(("stripe", "frame")),
        P(("stripe", "frame"), None),
        P(("stripe", "frame")),
        P(),
    )
    return jax.shard_map(
        per_device,
        mesh=mesh,
        in_specs=placed,
        out_specs=(P(("stripe", "frame"), None, None), P(("stripe", "frame"), None)),
        check_vma=False,
    )
```

```python
import math

import jax
import jax.numpy as jnp
from jax import lax
from jax.sharding import PartitionSpec as P


def dft_table(rows, columns, pixels):
    lo_count = 64 if rows % 64 == 0 else 1
    hi_count = rows // lo_count
    c = jnp.arange(columns, dtype=jnp.int32)
    scale = 2.0 * math.pi / pixels
    hi = jnp.arange(hi_count, dtype=jnp.int32)
    lo = jnp.arange(lo_count, dtype=jnp.int32)
    phase_hi = (hi[:, None] * lo_count * c[None, :] % pixels).astype(jnp.float32) * scale
    phase_lo = (lo[:, None] * c[None, :] % pixels).astype(jnp.float32) * scale
    c1, s1 = jnp.cos(phase_hi)[:, None, :], jnp.sin(phase_hi)[:, None, :]
    c2, s2 = jnp.cos(phase_lo)[None, :, :], jnp.sin(phase_lo)[None, :, :]
    cos_t = (c1 * c2 - s1 * s2).reshape(rows, columns)
    nsin_t = (-(s1 * c2 + c1 * s2)).reshape(rows, columns)
    return cos_t.astype(jnp.bfloat16), nsin_t.astype(jnp.bfloat16)


def shift_rows(frame_img, amount):
    pixels = frame_img.shape[-1]
    doubled = jnp.concatenate([frame_img, frame_img], axis=1)
    start = pixels - lax.rem(amount, pixels)
    return lax.dynamic_slice_in_dim(doubled, start, pixels, axis=1)


def stripe_exchange(blocks, axis):
    count = blocks.shape[0]
    me = lax.axis_index(axis)
    received = [lax.dynamic_index_in_dim(blocks, me, 0, keepdims=False)]
    for d in range(1, count):
        outgoing = lax.dynamic_index_in_dim(blocks, lax.rem(me + d, count), 0, keepdims=False)
        pairs = [(i, (i + d) % count) for i in range(count)]
        received.append(lax.ppermute(outgoing, axis, pairs))
    return jnp.stack(received)


def stripe_return(blocks, axis):
    count = blocks.shape[0]
    total = blocks[0]
    for d in range(1, count):
        pairs = [(i, (i - d) % count) for i in range(count)]
        total = total + lax.ppermute(blocks[d], axis, pairs)
    return total


def per_device(reference_img, frames, shifts, dest_device, dest_row, visit_order):
    count_frames, band_rows, pixels = frames.shape
    steps = visit_order.shape[0]
    stripes = lax.axis_size("stripe")
    half = pixels // 2
    columns = min(pixels, half + 128)
    fwd_cos, fwd_sin = dft_table(pixels, columns, pixels)
    forward = jnp.concatenate([fwd_cos, fwd_sin], axis=1)
    inv_cos, inv_sin = dft_table(columns, pixels, pixels)
    inverse = jnp.concatenate([inv_cos, inv_sin], axis=0)
    col = jnp.arange(columns, dtype=jnp.int32)
    weight = jnp.where((col == 0) | (col == half), 1.0, jnp.where(col < half, 2.0, 0.0))

    chunk = band_rows // stripes
    frame_part = frames.reshape(count_frames, stripes, chunk, pixels).transpose(1, 0, 2, 3)
    frame_part = frame_part.reshape(stripes, count_frames * chunk, pixels)
    band_part = reference_img.reshape(stripes, chunk, pixels)
    outbound = jnp.concatenate([frame_part, band_part], axis=1)
    inbound = stripe_exchange(outbound, "stripe")
    frame_rows_in = inbound[:, : count_frames * chunk].reshape(stripes * count_frames * chunk, pixels)
    band_in = inbound[:, count_frames * chunk :]
    source = lax.rem(lax.axis_index("stripe") - visit_order + stripes, stripes)
    visited = jnp.take(band_in, source, axis=0, mode="clip").reshape(steps * chunk, pixels)

    spectra = jnp.dot(frame_rows_in, forward, preferred_element_type=jnp.float32).reshape(
        stripes, count_frames, 1, chunk, 2 * columns
    )
    spec_re = spectra[..., :columns]
    spec_im = spectra[..., columns:]
    band = (
        jnp.dot(visited, forward, preferred_element_type=jnp.float32)
        .astype(jnp.bfloat16)
        .astype(jnp.float32)
        .reshape(steps, chunk, 2 * columns)
    )
    band_re = band[..., :columns]
    band_im = band[..., columns:]
    frame_power = jnp.sum(spec_re * spec_re + spec_im * spec_im, axis=3)[:, :, 0]
    band_power = jnp.sum(band_re * band_re + band_im * band_im, axis=1)
    br = band_re[None, None]
    bi = band_im[None, None]
    cross_re = jnp.sum(spec_re * br, axis=3) + jnp.sum(spec_im * bi, axis=3)
    cross_im = jnp.sum(spec_im * br, axis=3) - jnp.sum(spec_re * bi, axis=3)
    partial = jnp.concatenate(
        [
            cross_re.reshape(stripes, count_frames * steps, columns),
            cross_im.reshape(stripes, count_frames * steps, columns),
            frame_power,
            jnp.broadcast_to(band_power[None], (stripes, steps, columns)),
        ],
        axis=1,
    )
    total = stripe_return(partial, "stripe")
    pairs = count_frames * steps
    cross_re = total[:pairs].reshape(count_frames, steps, columns)
    cross_im = total[pairs : 2 * pairs].reshape(count_frames, steps, columns)
    frame_power = total[2 * pairs : 2 * pairs + count_frames]
    band_power = total[2 * pairs + count_frames :]

    magnitude = jnp.sqrt(frame_power[:, None, :] * band_power[None, :, :] + 1e-06)
    coh_re = (cross_re / magnitude).astype(jnp.bfloat16).astype(jnp.float32) * weight
    coh_im = (cross_im / magnitude).astype(jnp.bfloat16).astype(jnp.float32) * weight
    coherence = jnp.concatenate([coh_re, coh_im], axis=2).astype(jnp.bfloat16)
    surface = jnp.dot(
        coherence.reshape(count_frames * steps, 2 * columns),
        inverse,
        preferred_element_type=jnp.float32,
    )
    correlation = (surface * math.sqrt(band_rows / pixels)).reshape(count_frames, steps, pixels)

    num_devices = lax.axis_size("stripe") * lax.axis_size("frame")
    frame_rows = count_frames * band_rows
    capacity = max(2, 2 * frame_rows // num_devices)
    placed = jnp.concatenate(
        [shift_rows(frames[f], shifts[f]) for f in range(count_frames)], axis=0
    )
    target_dev = dest_device[:, 0]
    onehot = (target_dev[:, None] == jnp.arange(num_devices, dtype=jnp.int32)[None, :]).astype(
        jnp.int32
    )
    row_rank = jnp.sum((jnp.cumsum(onehot, axis=0) - 1) * onehot, axis=1)
    slot_id = target_dev * capacity + row_rank
    select = slot_id[None, :] == jnp.arange(num_devices * capacity, dtype=jnp.int32)[:, None]
    select3 = select.reshape(num_devices, capacity, frame_rows)
    outgoing = jnp.einsum(
        "dsr,rx->dsx", select3.astype(jnp.bfloat16), placed, preferred_element_type=jnp.float32
    ).astype(jnp.bfloat16)
    filled = jnp.any(select3, axis=2)
    local_row = jnp.sum(jnp.where(select3, dest_row[None, None, :], 0), axis=2)
    out_index = jnp.where(filled, local_row, -1).astype(jnp.float32).astype(jnp.bfloat16)
    lanes = 128
    index_cols = jnp.broadcast_to(out_index[:, :, None], (num_devices, capacity, lanes))
    packed = jnp.concatenate([outgoing, index_cols], axis=2)
    received = lax.all_to_all(packed, ("stripe", "frame"), split_axis=0, concat_axis=0, tiled=True)
    incoming = received[:, :, :pixels]
    index_f = received[:, :, pixels].astype(jnp.float32)
    hits = index_f[None, :, :] == jnp.arange(band_rows, dtype=jnp.float32)[:, None, None]
    landed = jnp.einsum(
        "tps,psx->tx", hits.astype(jnp.bfloat16), incoming, preferred_element_type=jnp.float32
    )
    land_count = jnp.sum(hits.astype(jnp.float32), axis=(1, 2))
    blended = (reference_img.astype(jnp.float32) + landed) / (1.0 + land_count[:, None])
    return (correlation, blended)


def solution(mesh):
    placed = (
        P(("stripe", "frame"), None),
        P(("stripe", "frame"), None, None),
        P(("stripe", "frame")),
        P(("stripe", "frame"), None),
        P(("stripe", "frame")),
        P(),
    )
    return jax.shard_map(
        per_device,
        mesh=mesh,
        in_specs=placed,
        out_specs=(P(("stripe", "frame"), None, None), P(("stripe", "frame"), None)),
        check_vma=False,
    )
```

```python
import math

import jax
import jax.numpy as jnp
from jax import lax
from jax.sharding import PartitionSpec as P


def dft_table(rows, columns, pixels):
    lo_count = 64 if rows % 64 == 0 else 1
    hi_count = rows // lo_count
    c = jnp.arange(columns, dtype=jnp.int32)
    scale = 2.0 * math.pi / pixels
    hi = jnp.arange(hi_count, dtype=jnp.int32)
    lo = jnp.arange(lo_count, dtype=jnp.int32)
    phase_hi = (hi[:, None] * lo_count * c[None, :] % pixels).astype(jnp.float32) * scale
    phase_lo = (lo[:, None] * c[None, :] % pixels).astype(jnp.float32) * scale
    c1, s1 = jnp.cos(phase_hi)[:, None, :], jnp.sin(phase_hi)[:, None, :]
    c2, s2 = jnp.cos(phase_lo)[None, :, :], jnp.sin(phase_lo)[None, :, :]
    cos_t = (c1 * c2 - s1 * s2).reshape(rows, columns)
    nsin_t = (-(s1 * c2 + c1 * s2)).reshape(rows, columns)
    return cos_t.astype(jnp.bfloat16), nsin_t.astype(jnp.bfloat16)


def shift_rows(frame_img, amount):
    pixels = frame_img.shape[-1]
    doubled = jnp.concatenate([frame_img, frame_img], axis=1)
    start = pixels - lax.rem(amount, pixels)
    return lax.dynamic_slice_in_dim(doubled, start, pixels, axis=1)


def per_device(reference_img, frames, shifts, dest_device, dest_row, visit_order):
    count_frames, band_rows, pixels = frames.shape
    steps = visit_order.shape[0]
    half = pixels // 2
    columns = min(pixels, half + 128)
    fwd_cos, fwd_sin = dft_table(pixels, columns, pixels)
    forward = jnp.concatenate([fwd_cos, fwd_sin], axis=1)
    col = jnp.arange(columns, dtype=jnp.int32)
    weight = jnp.where((col == 0) | (col == half), 1.0, jnp.where(col < half, 2.0, 0.0))

    stripes = lax.axis_size("stripe")
    split = (band_rows * 5 // 8) // 16 * 16 if band_rows % 16 == 0 else band_rows
    bounds = [(0, split)] + ([(split, band_rows)] if split < band_rows else [])
    gathered = [lax.all_gather(reference_img[:split], "stripe")]
    if split < band_rows:
        rest = reference_img[split:]
        spread = jnp.broadcast_to(rest[None], (stripes,) + rest.shape)
        gathered.append(lax.all_to_all(spread, "stripe", split_axis=0, concat_axis=0, tiled=True))

    frame_flat = frames.reshape(count_frames * band_rows, pixels)
    spectra = jnp.dot(frame_flat, forward, preferred_element_type=jnp.float32).reshape(
        count_frames, band_rows, 2 * columns
    )
    spec_re = spectra[:, :, :columns]
    spec_im = spectra[:, :, columns:]
    frame_power = jnp.sum(spec_re * spec_re + spec_im * spec_im, axis=1)

    band_power = 0.0
    cross_re = 0.0
    cross_im = 0.0
    for p, (lo, hi) in enumerate(bounds):
        piece_rows = hi - lo
        visited = jnp.take(gathered[p], visit_order, axis=0, mode="clip")
        band = (
            jnp.dot(
                visited.reshape(steps * piece_rows, pixels),
                forward,
                preferred_element_type=jnp.float32,
            )
            .astype(jnp.bfloat16)
            .astype(jnp.float32)
            .reshape(steps, piece_rows, 2 * columns)
        )
        band_re = band[:, :, :columns]
        band_im = band[:, :, columns:]
        band_power = band_power + jnp.sum(band_re * band_re + band_im * band_im, axis=1)
        fr = spec_re[:, None, lo:hi]
        fi = spec_im[:, None, lo:hi]
        br = band_re[None]
        bi = band_im[None]
        cross_re = cross_re + (jnp.sum(fr * br, axis=2) + jnp.sum(fi * bi, axis=2))
        cross_im = cross_im + (jnp.sum(fi * br, axis=2) - jnp.sum(fr * bi, axis=2))
    magnitude = jnp.sqrt(frame_power[:, None, :] * band_power[None, :, :] + 1e-06)
    coh_re = (cross_re / magnitude).astype(jnp.bfloat16).astype(jnp.float32) * weight
    coh_im = (cross_im / magnitude).astype(jnp.bfloat16).astype(jnp.float32) * weight
    coherence = jnp.concatenate([coh_re, coh_im], axis=2).astype(jnp.bfloat16)
    surface = lax.dot_general(
        coherence.reshape(count_frames * steps, 2 * columns),
        forward,
        (((1,), (1,)), ((), ())),
        preferred_element_type=jnp.float32,
    )
    correlation = (surface * math.sqrt(band_rows / pixels)).reshape(count_frames, steps, pixels)

    num_devices = lax.axis_size("stripe") * lax.axis_size("frame")
    frame_rows = count_frames * band_rows
    capacity = max(2, 2 * frame_rows // num_devices)
    placed = jnp.concatenate(
        [shift_rows(frames[f], shifts[f]) for f in range(count_frames)], axis=0
    )
    target_dev = dest_device[:, 0]
    onehot = (target_dev[:, None] == jnp.arange(num_devices, dtype=jnp.int32)[None, :]).astype(
        jnp.int32
    )
    row_rank = jnp.sum((jnp.cumsum(onehot, axis=0) - 1) * onehot, axis=1)
    slot_id = target_dev * capacity + row_rank
    select = slot_id[None, :] == jnp.arange(num_devices * capacity, dtype=jnp.int32)[:, None]
    select3 = select.reshape(num_devices, capacity, frame_rows)
    outgoing = jnp.einsum(
        "dsr,rx->dsx", select3.astype(jnp.bfloat16), placed, preferred_element_type=jnp.float32
    ).astype(jnp.bfloat16)
    filled = jnp.any(select3, axis=2)
    local_row = jnp.sum(jnp.where(select3, dest_row[None, None, :], 0), axis=2)
    out_index = jnp.where(filled, local_row, -1).astype(jnp.float32).astype(jnp.bfloat16)
    lanes = 128
    index_cols = jnp.broadcast_to(out_index[:, :, None], (num_devices, capacity, lanes))
    packed = jnp.concatenate([outgoing, index_cols], axis=2)
    received = lax.all_to_all(packed, ("stripe", "frame"), split_axis=0, concat_axis=0, tiled=True)
    incoming = received[:, :, :pixels]
    index_f = received[:, :, pixels].astype(jnp.float32)
    hits = index_f[None, :, :] == jnp.arange(band_rows, dtype=jnp.float32)[:, None, None]
    landed = jnp.einsum(
        "tps,psx->tx", hits.astype(jnp.bfloat16), incoming, preferred_element_type=jnp.float32
    )
    land_count = jnp.sum(hits.astype(jnp.float32), axis=(1, 2))
    blended = (reference_img.astype(jnp.float32) + landed) / (1.0 + land_count[:, None])
    return (correlation, blended)


def solution(mesh):
    placed = (
        P(("stripe", "frame"), None),
        P(("stripe", "frame"), None, None),
        P(("stripe", "frame")),
        P(("stripe", "frame"), None),
        P(("stripe", "frame")),
        P(),
    )
    return jax.shard_map(
        per_device,
        mesh=mesh,
        in_specs=placed,
        out_specs=(P(("stripe", "frame"), None, None), P(("stripe", "frame"), None)),
        check_vma=False,
    )
```

```python
import math

import jax
import jax.numpy as jnp
from jax import lax
from jax.sharding import PartitionSpec as P


def basis_halves(pixels, columns):
    lo_count = 64 if pixels % 64 == 0 else 1
    hi_count = pixels // lo_count
    u = jnp.arange(columns, dtype=jnp.int32)
    scale = 2.0 * math.pi / pixels
    hi = jnp.arange(hi_count, dtype=jnp.int32)
    lo = jnp.arange(lo_count, dtype=jnp.int32)
    phase_hi = (hi[:, None] * lo_count * u[None, :] % pixels).astype(jnp.float32) * scale
    phase_lo = (lo[:, None] * u[None, :] % pixels).astype(jnp.float32) * scale
    c1, s1 = jnp.cos(phase_hi)[:, None, :], jnp.sin(phase_hi)[:, None, :]
    c2, s2 = jnp.cos(phase_lo)[None, :, :], jnp.sin(phase_lo)[None, :, :]
    cos_t = (c1 * c2 - s1 * s2).reshape(pixels, columns).astype(jnp.bfloat16)
    nsin_t = (-(s1 * c2 + c1 * s2)).reshape(pixels, columns).astype(jnp.bfloat16)
    return cos_t, nsin_t


def shift_rows(frame_img, amount):
    pixels = frame_img.shape[-1]
    doubled = jnp.concatenate([frame_img, frame_img], axis=1)
    start = pixels - lax.rem(amount, pixels)
    return lax.dynamic_slice_in_dim(doubled, start, pixels, axis=1)


def per_device(reference_img, frames, shifts, dest_device, dest_row, visit_order):
    count_frames, band_rows, pixels = frames.shape
    steps = visit_order.shape[0]
    half = pixels // 2
    columns = min(pixels, half + 128)
    cos_t, nsin_t = basis_halves(pixels, columns)
    col = jnp.arange(columns, dtype=jnp.int32)
    weight = jnp.where((col == 0) | (col == half), 1.0, jnp.where(col < half, 2.0, 0.0))

    gathered = lax.all_gather(reference_img, "stripe")
    visited = jnp.take(gathered, visit_order, axis=0, mode="clip")

    frame_flat = frames.reshape(count_frames * band_rows, pixels)
    spec_re = jnp.dot(frame_flat, cos_t, preferred_element_type=jnp.float32).reshape(
        count_frames, band_rows, columns
    )
    spec_im = jnp.dot(frame_flat, nsin_t, preferred_element_type=jnp.float32).reshape(
        count_frames, band_rows, columns
    )
    frame_power = jnp.sum(spec_re * spec_re + spec_im * spec_im, axis=1)

    visited_flat = visited.reshape(steps * band_rows, pixels)
    band_re = (
        jnp.dot(visited_flat, cos_t, preferred_element_type=jnp.float32)
        .astype(jnp.bfloat16)
        .astype(jnp.float32)
        .reshape(steps, band_rows, columns)
    )
    band_im = (
        jnp.dot(visited_flat, nsin_t, preferred_element_type=jnp.float32)
        .astype(jnp.bfloat16)
        .astype(jnp.float32)
        .reshape(steps, band_rows, columns)
    )
    band_power = jnp.sum(band_re * band_re + band_im * band_im, axis=1)

    fr = spec_re[:, None]
    fi = spec_im[:, None]
    br = band_re[None]
    bi = band_im[None]
    cross_re = jnp.sum(fr * br, axis=2) + jnp.sum(fi * bi, axis=2)
    cross_im = jnp.sum(fi * br, axis=2) - jnp.sum(fr * bi, axis=2)
    magnitude = jnp.sqrt(frame_power[:, None, :] * band_power[None, :, :] + 1e-06)
    coh_re = (cross_re / magnitude).astype(jnp.bfloat16).astype(jnp.float32) * weight
    coh_im = (cross_im / magnitude).astype(jnp.bfloat16).astype(jnp.float32) * weight
    coh_re = coh_re.astype(jnp.bfloat16).reshape(count_frames * steps, columns)
    coh_im = coh_im.astype(jnp.bfloat16).reshape(count_frames * steps, columns)
    contract = (((1,), (1,)), ((), ()))
    surface = lax.dot_general(
        coh_re, cos_t, contract, preferred_element_type=jnp.float32
    ) + lax.dot_general(coh_im, nsin_t, contract, preferred_element_type=jnp.float32)
    correlation = (surface * math.sqrt(band_rows / pixels)).reshape(count_frames, steps, pixels)

    num_devices = lax.axis_size("stripe") * lax.axis_size("frame")
    frame_rows = count_frames * band_rows
    capacity = max(2, 2 * frame_rows // num_devices)
    placed = jnp.concatenate(
        [shift_rows(frames[f], shifts[f]) for f in range(count_frames)], axis=0
    )
    target_dev = dest_device[:, 0]
    onehot = (target_dev[:, None] == jnp.arange(num_devices, dtype=jnp.int32)[None, :]).astype(
        jnp.int32
    )
    row_rank = jnp.sum((jnp.cumsum(onehot, axis=0) - 1) * onehot, axis=1)
    slot_id = target_dev * capacity + row_rank
    select = slot_id[None, :] == jnp.arange(num_devices * capacity, dtype=jnp.int32)[:, None]
    select3 = select.reshape(num_devices, capacity, frame_rows)
    outgoing = jnp.einsum(
        "dsr,rx->dsx", select3.astype(jnp.bfloat16), placed, preferred_element_type=jnp.float32
    ).astype(jnp.bfloat16)
    filled = jnp.any(select3, axis=2)
    local_row = jnp.sum(jnp.where(select3, dest_row[None, None, :], 0), axis=2)
    out_index = jnp.where(filled, local_row, -1).astype(jnp.float32).astype(jnp.bfloat16)
    lanes = 128
    index_cols = jnp.broadcast_to(out_index[:, :, None], (num_devices, capacity, lanes))
    packed = jnp.concatenate([outgoing, index_cols], axis=2)
    packed, _ = lax.optimization_barrier((packed, gathered))
    received = lax.all_to_all(packed, ("stripe", "frame"), split_axis=0, concat_axis=0, tiled=True)
    incoming = received[:, :, :pixels]
    index_f = received[:, :, pixels].astype(jnp.float32)
    hits = index_f[None, :, :] == jnp.arange(band_rows, dtype=jnp.float32)[:, None, None]
    landed = jnp.einsum(
        "tps,psx->tx", hits.astype(jnp.bfloat16), incoming, preferred_element_type=jnp.float32
    )
    land_count = jnp.sum(hits.astype(jnp.float32), axis=(1, 2))
    blended = (reference_img.astype(jnp.float32) + landed) / (1.0 + land_count[:, None])
    return (correlation, blended)


def solution(mesh):
    placed = (
        P(("stripe", "frame"), None),
        P(("stripe", "frame"), None, None),
        P(("stripe", "frame")),
        P(("stripe", "frame"), None),
        P(("stripe", "frame")),
        P(),
    )
    return jax.shard_map(
        per_device,
        mesh=mesh,
        in_specs=placed,
        out_specs=(P(("stripe", "frame"), None, None), P(("stripe", "frame"), None)),
        check_vma=False,
    )
```

```python
import math

import jax
import jax.numpy as jnp
from jax import lax
from jax.sharding import PartitionSpec as P


def dft_table(rows, columns, pixels):
    lo_count = 64 if rows % 64 == 0 else 1
    hi_count = rows // lo_count
    c = jnp.arange(columns, dtype=jnp.int32)
    scale = 2.0 * math.pi / pixels
    hi = jnp.arange(hi_count, dtype=jnp.int32)
    lo = jnp.arange(lo_count, dtype=jnp.int32)
    phase_hi = (hi[:, None] * lo_count * c[None, :] % pixels).astype(jnp.float32) * scale
    phase_lo = (lo[:, None] * c[None, :] % pixels).astype(jnp.float32) * scale
    c1, s1 = jnp.cos(phase_hi)[:, None, :], jnp.sin(phase_hi)[:, None, :]
    c2, s2 = jnp.cos(phase_lo)[None, :, :], jnp.sin(phase_lo)[None, :, :]
    cos_t = (c1 * c2 - s1 * s2).reshape(rows, columns)
    nsin_t = (-(s1 * c2 + c1 * s2)).reshape(rows, columns)
    return cos_t.astype(jnp.bfloat16), nsin_t.astype(jnp.bfloat16)


def shift_rows(frame_img, amount):
    pixels = frame_img.shape[-1]
    doubled = jnp.concatenate([frame_img, frame_img], axis=1)
    start = pixels - lax.rem(amount, pixels)
    return lax.dynamic_slice_in_dim(doubled, start, pixels, axis=1)


def per_device(reference_img, frames, shifts, dest_device, dest_row, visit_order):
    count_frames, band_rows, pixels = frames.shape
    steps = visit_order.shape[0]
    stripes = lax.axis_size("stripe")
    half = pixels // 2
    columns = min(pixels, half + 128)
    fwd_cos, fwd_sin = dft_table(pixels, columns, pixels)
    forward = jnp.concatenate([fwd_cos, fwd_sin], axis=1)
    col = jnp.arange(columns, dtype=jnp.int32)
    weight = jnp.where((col == 0) | (col == half), 1.0, jnp.where(col < half, 2.0, 0.0))

    chunk = band_rows // stripes
    frame_part = frames.reshape(count_frames, stripes, chunk, pixels).transpose(1, 0, 2, 3)
    frame_part = frame_part.reshape(stripes, count_frames * chunk, pixels)
    band_part = reference_img.reshape(stripes, chunk, pixels)
    outbound = jnp.concatenate([frame_part, band_part], axis=1)
    inbound = lax.all_to_all(outbound, "stripe", split_axis=0, concat_axis=0, tiled=True)
    num_devices = lax.axis_size("stripe") * lax.axis_size("frame")
    frame_rows = count_frames * band_rows
    capacity = max(2, 2 * frame_rows // num_devices)
    placed = jnp.concatenate(
        [shift_rows(frames[f], shifts[f]) for f in range(count_frames)], axis=0
    )
    target_dev = dest_device[:, 0]
    onehot = (target_dev[:, None] == jnp.arange(num_devices, dtype=jnp.int32)[None, :]).astype(
        jnp.int32
    )
    row_rank = jnp.sum((jnp.cumsum(onehot, axis=0) - 1) * onehot, axis=1)
    slot_id = target_dev * capacity + row_rank
    select = slot_id[None, :] == jnp.arange(num_devices * capacity, dtype=jnp.int32)[:, None]
    select3 = select.reshape(num_devices, capacity, frame_rows)
    outgoing = jnp.einsum(
        "dsr,rx->dsx", select3.astype(jnp.bfloat16), placed, preferred_element_type=jnp.float32
    ).astype(jnp.bfloat16)
    filled = jnp.any(select3, axis=2)
    local_row = jnp.sum(jnp.where(select3, dest_row[None, None, :], 0), axis=2)
    out_index = jnp.where(filled, local_row, -1).astype(jnp.float32).astype(jnp.bfloat16)
    lanes = 128
    index_cols = jnp.broadcast_to(out_index[:, :, None], (num_devices, capacity, lanes))
    packed = jnp.concatenate([outgoing, index_cols], axis=2)
    packed, inbound = lax.optimization_barrier((packed, inbound))
    received = lax.all_to_all(packed, ("stripe", "frame"), split_axis=0, concat_axis=0, tiled=True)
    frame_rows_in = inbound[:, : count_frames * chunk].reshape(stripes * count_frames * chunk, pixels)
    band_in = inbound[:, count_frames * chunk :]
    visited = jnp.take(band_in, visit_order, axis=0, mode="clip").reshape(steps * chunk, pixels)

    spectra = jnp.dot(frame_rows_in, forward, preferred_element_type=jnp.float32).reshape(
        stripes, count_frames, 1, chunk, 2 * columns
    )
    spec_re = spectra[..., :columns]
    spec_im = spectra[..., columns:]
    band = (
        jnp.dot(visited, forward, preferred_element_type=jnp.float32)
        .astype(jnp.bfloat16)
        .astype(jnp.float32)
        .reshape(steps, chunk, 2 * columns)
    )
    band_re = band[..., :columns]
    band_im = band[..., columns:]
    frame_power = jnp.sum(spec_re * spec_re + spec_im * spec_im, axis=3)[:, :, 0]
    band_power = jnp.sum(band_re * band_re + band_im * band_im, axis=1)
    br = band_re[None, None]
    bi = band_im[None, None]
    cross_re = jnp.sum(spec_re * br, axis=3) + jnp.sum(spec_im * bi, axis=3)
    cross_im = jnp.sum(spec_im * br, axis=3) - jnp.sum(spec_re * bi, axis=3)
    partial = jnp.concatenate(
        [
            cross_re.reshape(stripes, count_frames * steps, columns),
            cross_im.reshape(stripes, count_frames * steps, columns),
            frame_power,
            jnp.broadcast_to(band_power[None], (stripes, steps, columns)),
        ],
        axis=1,
    )
    partial, received = lax.optimization_barrier((partial, received))
    total = jnp.sum(
        lax.all_to_all(partial, "stripe", split_axis=0, concat_axis=0, tiled=True), axis=0
    )
    pairs = count_frames * steps
    cross_re = total[:pairs].reshape(count_frames, steps, columns)
    cross_im = total[pairs : 2 * pairs].reshape(count_frames, steps, columns)
    frame_power = total[2 * pairs : 2 * pairs + count_frames]
    band_power = total[2 * pairs + count_frames :]

    magnitude = jnp.sqrt(frame_power[:, None, :] * band_power[None, :, :] + 1e-06)
    coh_re = (cross_re / magnitude).astype(jnp.bfloat16).astype(jnp.float32) * weight
    coh_im = (cross_im / magnitude).astype(jnp.bfloat16).astype(jnp.float32) * weight
    coherence = jnp.concatenate([coh_re, coh_im], axis=2).astype(jnp.bfloat16)
    surface = lax.dot_general(
        coherence.reshape(count_frames * steps, 2 * columns),
        forward,
        (((1,), (1,)), ((), ())),
        preferred_element_type=jnp.float32,
    )
    correlation = (surface * math.sqrt(band_rows / pixels)).reshape(count_frames, steps, pixels)

    incoming = received[:, :, :pixels]
    index_f = received[:, :, pixels].astype(jnp.float32)
    hits = index_f[None, :, :] == jnp.arange(band_rows, dtype=jnp.float32)[:, None, None]
    landed = jnp.einsum(
        "tps,psx->tx", hits.astype(jnp.bfloat16), incoming, preferred_element_type=jnp.float32
    )
    land_count = jnp.sum(hits.astype(jnp.float32), axis=(1, 2))
    blended = (reference_img.astype(jnp.float32) + landed) / (1.0 + land_count[:, None])
    return (correlation, blended)


def solution(mesh):
    placed = (
        P(("stripe", "frame"), None),
        P(("stripe", "frame"), None, None),
        P(("stripe", "frame")),
        P(("stripe", "frame"), None),
        P(("stripe", "frame")),
        P(),
    )
    return jax.shard_map(
        per_device,
        mesh=mesh,
        in_specs=placed,
        out_specs=(P(("stripe", "frame"), None, None), P(("stripe", "frame"), None)),
        check_vma=False,
    )
```

```python
import math

import jax
import jax.numpy as jnp
from jax import lax
from jax.sharding import PartitionSpec as P


def dft_table(rows, columns, pixels):
    lo_count = 64 if rows % 64 == 0 else 1
    hi_count = rows // lo_count
    c = jnp.arange(columns, dtype=jnp.int32)
    scale = 2.0 * math.pi / pixels
    hi = jnp.arange(hi_count, dtype=jnp.int32)
    lo = jnp.arange(lo_count, dtype=jnp.int32)
    phase_hi = (hi[:, None] * lo_count * c[None, :] % pixels).astype(jnp.float32) * scale
    phase_lo = (lo[:, None] * c[None, :] % pixels).astype(jnp.float32) * scale
    c1, s1 = jnp.cos(phase_hi)[:, None, :], jnp.sin(phase_hi)[:, None, :]
    c2, s2 = jnp.cos(phase_lo)[None, :, :], jnp.sin(phase_lo)[None, :, :]
    cos_t = (c1 * c2 - s1 * s2).reshape(rows, columns)
    nsin_t = (-(s1 * c2 + c1 * s2)).reshape(rows, columns)
    return cos_t.astype(jnp.bfloat16), nsin_t.astype(jnp.bfloat16)


def shift_rows(frame_img, amount):
    pixels = frame_img.shape[-1]
    doubled = jnp.concatenate([frame_img, frame_img], axis=1)
    start = pixels - lax.rem(amount, pixels)
    return lax.dynamic_slice_in_dim(doubled, start, pixels, axis=1)


def per_device(reference_img, frames, shifts, dest_device, dest_row, visit_order):
    count_frames, band_rows, pixels = frames.shape
    steps = visit_order.shape[0]
    stripes = lax.axis_size("stripe")
    half = pixels // 2
    columns = min(pixels, half + 128)
    fwd_cos, fwd_sin = dft_table(pixels, columns, pixels)
    forward = jnp.concatenate([fwd_cos, fwd_sin], axis=1)
    col = jnp.arange(columns, dtype=jnp.int32)
    weight = jnp.where((col == 0) | (col == half), 1.0, jnp.where(col < half, 2.0, 0.0))

    chunk = band_rows // stripes
    frame_part = frames.reshape(count_frames, stripes, chunk, pixels).transpose(1, 0, 2, 3)
    frame_part = frame_part.reshape(stripes, count_frames * chunk, pixels)
    band_part = reference_img.reshape(stripes, chunk, pixels)
    outbound = jnp.concatenate([frame_part, band_part], axis=1)
    inbound = lax.all_to_all(outbound, "stripe", split_axis=0, concat_axis=0, tiled=True)
    num_devices = lax.axis_size("stripe") * lax.axis_size("frame")
    frame_rows = count_frames * band_rows
    capacity = max(2, 2 * frame_rows // num_devices)
    placed = jnp.concatenate(
        [shift_rows(frames[f], shifts[f]) for f in range(count_frames)], axis=0
    )
    target_dev = dest_device[:, 0]
    onehot = (target_dev[:, None] == jnp.arange(num_devices, dtype=jnp.int32)[None, :]).astype(
        jnp.int32
    )
    row_rank = jnp.sum((jnp.cumsum(onehot, axis=0) - 1) * onehot, axis=1)
    slot_id = target_dev * capacity + row_rank
    select = slot_id[None, :] == jnp.arange(num_devices * capacity, dtype=jnp.int32)[:, None]
    select3 = select.reshape(num_devices, capacity, frame_rows)
    outgoing = jnp.einsum(
        "dsr,rx->dsx", select3.astype(jnp.bfloat16), placed, preferred_element_type=jnp.float32
    ).astype(jnp.bfloat16)
    filled = jnp.any(select3, axis=2)
    local_row = jnp.sum(jnp.where(select3, dest_row[None, None, :], 0), axis=2)
    out_index = jnp.where(filled, local_row, -1).astype(jnp.float32).astype(jnp.bfloat16)
    lanes = 128
    index_cols = jnp.broadcast_to(out_index[:, :, None], (num_devices, capacity, lanes))
    packed = jnp.concatenate([outgoing, index_cols], axis=2)
    packed, inbound = lax.optimization_barrier((packed, inbound))
    received = lax.all_to_all(packed, ("stripe", "frame"), split_axis=0, concat_axis=0, tiled=True)
    frame_rows_in = (
        inbound[:, : count_frames * chunk]
        .reshape(stripes, count_frames, chunk, pixels)
        .transpose(2, 0, 1, 3)
        .reshape(chunk * stripes * count_frames, pixels)
    )
    band_in = inbound[:, count_frames * chunk :]
    visited = jnp.take(band_in, visit_order, axis=0, mode="clip").transpose(1, 0, 2)
    visited = visited.reshape(chunk * steps, pixels)

    spectra = jnp.dot(frame_rows_in, forward, preferred_element_type=jnp.float32).reshape(
        chunk, stripes * count_frames, 1, 2 * columns
    )
    spec_re = spectra[..., :columns]
    spec_im = spectra[..., columns:]
    band = (
        jnp.dot(visited, forward, preferred_element_type=jnp.float32)
        .astype(jnp.bfloat16)
        .astype(jnp.float32)
        .reshape(chunk, 1, steps, 2 * columns)
    )
    band_re = band[..., :columns]
    band_im = band[..., columns:]
    frame_power = jnp.sum(spec_re * spec_re + spec_im * spec_im, axis=0)[:, 0]
    band_power = jnp.sum(band_re * band_re + band_im * band_im, axis=0)[0]
    cross_re = jnp.sum(spec_re * band_re + spec_im * band_im, axis=0)
    cross_im = jnp.sum(spec_im * band_re - spec_re * band_im, axis=0)
    frame_power = frame_power.reshape(stripes, count_frames, columns)
    partial = jnp.concatenate(
        [
            cross_re.reshape(stripes, count_frames * steps, columns),
            cross_im.reshape(stripes, count_frames * steps, columns),
            frame_power,
            jnp.broadcast_to(band_power[None], (stripes, steps, columns)),
        ],
        axis=1,
    )
    partial, received = lax.optimization_barrier((partial, received))
    total = jnp.sum(
        lax.all_to_all(partial, "stripe", split_axis=0, concat_axis=0, tiled=True), axis=0
    )
    pairs = count_frames * steps
    cross_re = total[:pairs].reshape(count_frames, steps, columns)
    cross_im = total[pairs : 2 * pairs].reshape(count_frames, steps, columns)
    frame_power = total[2 * pairs : 2 * pairs + count_frames]
    band_power = total[2 * pairs + count_frames :]

    magnitude = jnp.sqrt(frame_power[:, None, :] * band_power[None, :, :] + 1e-06)
    coh_re = (cross_re / magnitude).astype(jnp.bfloat16).astype(jnp.float32) * weight
    coh_im = (cross_im / magnitude).astype(jnp.bfloat16).astype(jnp.float32) * weight
    coherence = jnp.concatenate([coh_re, coh_im], axis=2).astype(jnp.bfloat16)
    surface = lax.dot_general(
        coherence.reshape(count_frames * steps, 2 * columns),
        forward,
        (((1,), (1,)), ((), ())),
        preferred_element_type=jnp.float32,
    )
    correlation = (surface * math.sqrt(band_rows / pixels)).reshape(count_frames, steps, pixels)

    incoming = received[:, :, :pixels]
    index_f = received[:, :, pixels].astype(jnp.float32)
    hits = index_f[None, :, :] == jnp.arange(band_rows, dtype=jnp.float32)[:, None, None]
    landed = jnp.einsum(
        "tps,psx->tx", hits.astype(jnp.bfloat16), incoming, preferred_element_type=jnp.float32
    )
    land_count = jnp.sum(hits.astype(jnp.float32), axis=(1, 2))
    blended = (reference_img.astype(jnp.float32) + landed) / (1.0 + land_count[:, None])
    return (correlation, blended)


def solution(mesh):
    placed = (
        P(("stripe", "frame"), None),
        P(("stripe", "frame"), None, None),
        P(("stripe", "frame")),
        P(("stripe", "frame"), None),
        P(("stripe", "frame")),
        P(),
    )
    return jax.shard_map(
        per_device,
        mesh=mesh,
        in_specs=placed,
        out_specs=(P(("stripe", "frame"), None, None), P(("stripe", "frame"), None)),
        check_vma=False,
    )
```

```python
import math

import jax
import jax.numpy as jnp
from jax import lax
from jax.sharding import PartitionSpec as P


def dft_table(rows, columns, pixels):
    lo_count = 64 if rows % 64 == 0 else 1
    hi_count = rows // lo_count
    c = jnp.arange(columns, dtype=jnp.int32)
    scale = 2.0 * math.pi / pixels
    hi = jnp.arange(hi_count, dtype=jnp.int32)
    lo = jnp.arange(lo_count, dtype=jnp.int32)
    phase_hi = (hi[:, None] * lo_count * c[None, :] % pixels).astype(jnp.float32) * scale
    phase_lo = (lo[:, None] * c[None, :] % pixels).astype(jnp.float32) * scale
    c1, s1 = jnp.cos(phase_hi)[:, None, :], jnp.sin(phase_hi)[:, None, :]
    c2, s2 = jnp.cos(phase_lo)[None, :, :], jnp.sin(phase_lo)[None, :, :]
    cos_t = (c1 * c2 - s1 * s2).reshape(rows, columns)
    nsin_t = (-(s1 * c2 + c1 * s2)).reshape(rows, columns)
    return cos_t.astype(jnp.bfloat16), nsin_t.astype(jnp.bfloat16)


def shift_rows(frame_img, amount):
    pixels = frame_img.shape[-1]
    doubled = jnp.concatenate([frame_img, frame_img], axis=1)
    start = pixels - lax.rem(amount, pixels)
    return lax.dynamic_slice_in_dim(doubled, start, pixels, axis=1)


def per_device(reference_img, frames, shifts, dest_device, dest_row, visit_order):
    count_frames, band_rows, pixels = frames.shape
    steps = visit_order.shape[0]
    stripes = lax.axis_size("stripe")
    half = pixels // 2
    columns = min(pixels, half + 128)
    fwd_cos, fwd_sin = dft_table(pixels, columns, pixels)
    forward = jnp.concatenate([fwd_cos, fwd_sin], axis=1)
    col = jnp.arange(columns, dtype=jnp.int32)
    weight = jnp.where((col == 0) | (col == half), 1.0, jnp.where(col < half, 2.0, 0.0))

    chunk = band_rows // stripes
    frame_part = frames.reshape(count_frames, stripes, chunk, pixels).transpose(1, 0, 2, 3)
    frame_part = frame_part.reshape(stripes, count_frames * chunk, pixels)
    band_part = reference_img.reshape(stripes, chunk, pixels)
    outbound = jnp.concatenate([frame_part, band_part], axis=1)
    inbound = lax.all_to_all(outbound, "stripe", split_axis=0, concat_axis=0, tiled=True)
    num_devices = lax.axis_size("stripe") * lax.axis_size("frame")
    frame_rows = count_frames * band_rows
    capacity = max(2, 2 * frame_rows // num_devices)
    placed = jnp.concatenate(
        [shift_rows(frames[f], shifts[f]) for f in range(count_frames)], axis=0
    )
    target_dev = dest_device[:, 0]
    onehot = (target_dev[:, None] == jnp.arange(num_devices, dtype=jnp.int32)[None, :]).astype(
        jnp.int32
    )
    row_rank = jnp.sum((jnp.cumsum(onehot, axis=0) - 1) * onehot, axis=1)
    slot_id = target_dev * capacity + row_rank
    select = slot_id[None, :] == jnp.arange(num_devices * capacity, dtype=jnp.int32)[:, None]
    select3 = select.reshape(num_devices, capacity, frame_rows)
    outgoing = jnp.einsum(
        "dsr,rx->dsx", select3.astype(jnp.bfloat16), placed, preferred_element_type=jnp.float32
    ).astype(jnp.bfloat16)
    filled = jnp.any(select3, axis=2)
    local_row = jnp.sum(jnp.where(select3, dest_row[None, None, :], 0), axis=2)
    out_index = jnp.where(filled, local_row, -1).astype(jnp.float32).astype(jnp.bfloat16)
    lanes = 128
    index_cols = jnp.broadcast_to(out_index[:, :, None], (num_devices, capacity, lanes))
    packed = jnp.concatenate([outgoing, index_cols], axis=2)
    received = lax.all_to_all(packed, ("stripe", "frame"), split_axis=0, concat_axis=0, tiled=True)
    frame_rows_in = (
        inbound[:, : count_frames * chunk]
        .reshape(stripes, count_frames, chunk, pixels)
        .transpose(2, 0, 1, 3)
        .reshape(chunk * stripes * count_frames, pixels)
    )
    band_in = inbound[:, count_frames * chunk :]
    visited = jnp.take(band_in, visit_order, axis=0, mode="clip").transpose(1, 0, 2)
    visited = visited.reshape(chunk * steps, pixels)

    spectra = jnp.dot(frame_rows_in, forward, preferred_element_type=jnp.float32).reshape(
        chunk, stripes * count_frames, 1, 2 * columns
    )
    spec_re = spectra[..., :columns]
    spec_im = spectra[..., columns:]
    band = (
        jnp.dot(visited, forward, preferred_element_type=jnp.float32)
        .astype(jnp.bfloat16)
        .astype(jnp.float32)
        .reshape(chunk, 1, steps, 2 * columns)
    )
    band_re = band[..., :columns]
    band_im = band[..., columns:]
    frame_power = jnp.sum(spec_re * spec_re + spec_im * spec_im, axis=0)[:, 0]
    band_power = jnp.sum(band_re * band_re + band_im * band_im, axis=0)[0]
    cross_re = jnp.sum(spec_re * band_re + spec_im * band_im, axis=0)
    cross_im = jnp.sum(spec_im * band_re - spec_re * band_im, axis=0)
    frame_power = frame_power.reshape(stripes, count_frames, columns)
    partial = jnp.concatenate(
        [
            cross_re.reshape(stripes, count_frames * steps, columns),
            cross_im.reshape(stripes, count_frames * steps, columns),
            frame_power,
            jnp.broadcast_to(band_power[None], (stripes, steps, columns)),
        ],
        axis=1,
    )
    partial, received = lax.optimization_barrier((partial, received))
    total = jnp.sum(
        lax.all_to_all(partial, "stripe", split_axis=0, concat_axis=0, tiled=True), axis=0
    )
    pairs = count_frames * steps
    cross_re = total[:pairs].reshape(count_frames, steps, columns)
    cross_im = total[pairs : 2 * pairs].reshape(count_frames, steps, columns)
    frame_power = total[2 * pairs : 2 * pairs + count_frames]
    band_power = total[2 * pairs + count_frames :]

    magnitude = jnp.sqrt(frame_power[:, None, :] * band_power[None, :, :] + 1e-06)
    coh_re = (cross_re / magnitude).astype(jnp.bfloat16).astype(jnp.float32) * weight
    coh_im = (cross_im / magnitude).astype(jnp.bfloat16).astype(jnp.float32) * weight
    coherence = jnp.concatenate([coh_re, coh_im], axis=2).astype(jnp.bfloat16)
    surface = lax.dot_general(
        coherence.reshape(count_frames * steps, 2 * columns),
        forward,
        (((1,), (1,)), ((), ())),
        preferred_element_type=jnp.float32,
    )
    correlation = (surface * math.sqrt(band_rows / pixels)).reshape(count_frames, steps, pixels)

    incoming = received[:, :, :pixels]
    index_f = received[:, :, pixels].astype(jnp.float32)
    hits = index_f[None, :, :] == jnp.arange(band_rows, dtype=jnp.float32)[:, None, None]
    landed = jnp.einsum(
        "tps,psx->tx", hits.astype(jnp.bfloat16), incoming, preferred_element_type=jnp.float32
    )
    land_count = jnp.sum(hits.astype(jnp.float32), axis=(1, 2))
    blended = (reference_img.astype(jnp.float32) + landed) / (1.0 + land_count[:, None])
    return (correlation, blended)


def solution(mesh):
    placed = (
        P(("stripe", "frame"), None),
        P(("stripe", "frame"), None, None),
        P(("stripe", "frame")),
        P(("stripe", "frame"), None),
        P(("stripe", "frame")),
        P(),
    )
    return jax.shard_map(
        per_device,
        mesh=mesh,
        in_specs=placed,
        out_specs=(P(("stripe", "frame"), None, None), P(("stripe", "frame"), None)),
        check_vma=False,
    )
```

```python
import math

import jax
import jax.numpy as jnp
from jax import lax
from jax.sharding import PartitionSpec as P


def dft_table(rows, columns, pixels):
    lo_count = 64 if rows % 64 == 0 else 1
    hi_count = rows // lo_count
    c = jnp.arange(columns, dtype=jnp.int32)
    scale = 2.0 * math.pi / pixels
    hi = jnp.arange(hi_count, dtype=jnp.int32)
    lo = jnp.arange(lo_count, dtype=jnp.int32)
    phase_hi = (hi[:, None] * lo_count * c[None, :] % pixels).astype(jnp.float32) * scale
    phase_lo = (lo[:, None] * c[None, :] % pixels).astype(jnp.float32) * scale
    c1, s1 = jnp.cos(phase_hi)[:, None, :], jnp.sin(phase_hi)[:, None, :]
    c2, s2 = jnp.cos(phase_lo)[None, :, :], jnp.sin(phase_lo)[None, :, :]
    cos_t = (c1 * c2 - s1 * s2).reshape(rows, columns)
    nsin_t = (-(s1 * c2 + c1 * s2)).reshape(rows, columns)
    return cos_t.astype(jnp.bfloat16), nsin_t.astype(jnp.bfloat16)


def shift_rows(frame_img, amount):
    pixels = frame_img.shape[-1]
    doubled = jnp.concatenate([frame_img, frame_img], axis=1)
    start = pixels - lax.rem(amount, pixels)
    return lax.dynamic_slice_in_dim(doubled, start, pixels, axis=1)


def per_device(reference_img, frames, shifts, dest_device, dest_row, visit_order):
    count_frames, band_rows, pixels = frames.shape
    steps = visit_order.shape[0]
    stripes = lax.axis_size("stripe")
    half = pixels // 2
    columns = min(pixels, half + 128)
    fwd_cos, fwd_sin = dft_table(pixels, columns, pixels)
    forward = jnp.concatenate([fwd_cos, fwd_sin], axis=1)
    col = jnp.arange(columns, dtype=jnp.int32)
    weight = jnp.where((col == 0) | (col == half), 1.0, jnp.where(col < half, 2.0, 0.0))

    chunk = band_rows // stripes
    frame_part = frames.reshape(count_frames, stripes, chunk, pixels).transpose(1, 0, 2, 3)
    frame_part = frame_part.reshape(stripes, count_frames * chunk, pixels)
    band_part = reference_img.reshape(stripes, chunk, pixels)
    outbound = jnp.concatenate([frame_part, band_part], axis=1)
    inbound = lax.all_to_all(outbound, "stripe", split_axis=0, concat_axis=0, tiled=True)
    num_devices = lax.axis_size("stripe") * lax.axis_size("frame")
    frame_rows = count_frames * band_rows
    capacity = max(2, 2 * frame_rows // num_devices)
    placed = jnp.concatenate(
        [shift_rows(frames[f], shifts[f]) for f in range(count_frames)], axis=0
    )
    target_dev = dest_device[:, 0]
    onehot = (target_dev[:, None] == jnp.arange(num_devices, dtype=jnp.int32)[None, :]).astype(
        jnp.int32
    )
    row_rank = jnp.sum((jnp.cumsum(onehot, axis=0) - 1) * onehot, axis=1)
    slot_id = target_dev * capacity + row_rank
    select = slot_id[None, :] == jnp.arange(num_devices * capacity, dtype=jnp.int32)[:, None]
    select3 = select.reshape(num_devices, capacity, frame_rows)
    outgoing = jnp.einsum(
        "dsr,rx->dsx", select3.astype(jnp.bfloat16), placed, preferred_element_type=jnp.float32
    ).astype(jnp.bfloat16)
    filled = jnp.any(select3, axis=2)
    local_row = jnp.sum(jnp.where(select3, dest_row[None, None, :], 0), axis=2)
    out_index = jnp.where(filled, local_row, -1).astype(jnp.float32).astype(jnp.bfloat16)
    lanes = 128
    index_cols = jnp.broadcast_to(out_index[:, :, None], (num_devices, capacity, lanes))
    packed = jnp.concatenate([outgoing, index_cols], axis=2)
    received = lax.all_to_all(packed, ("stripe", "frame"), split_axis=0, concat_axis=0, tiled=True)
    frame_rows_in = (
        inbound[:, : count_frames * chunk]
        .reshape(stripes, count_frames, chunk, pixels)
        .transpose(2, 0, 1, 3)
        .reshape(chunk * stripes * count_frames, pixels)
    )
    band_in = inbound[:, count_frames * chunk :]
    visited = jnp.take(band_in, visit_order, axis=0, mode="clip").transpose(1, 0, 2)
    visited = visited.reshape(chunk * steps, pixels)

    spectra = jnp.dot(frame_rows_in, forward, preferred_element_type=jnp.float32).reshape(
        chunk, stripes * count_frames, 1, 2 * columns
    )
    spec_re = spectra[..., :columns]
    spec_im = spectra[..., columns:]
    band = (
        jnp.dot(visited, forward, preferred_element_type=jnp.float32)
        .astype(jnp.bfloat16)
        .astype(jnp.float32)
        .reshape(chunk, 1, steps, 2 * columns)
    )
    band_re = band[..., :columns]
    band_im = band[..., columns:]
    frame_power = jnp.sum(spec_re * spec_re + spec_im * spec_im, axis=0)[:, 0]
    band_power = jnp.sum(band_re * band_re + band_im * band_im, axis=0)[0]
    cross_re = jnp.sum(spec_re * band_re + spec_im * band_im, axis=0)
    cross_im = jnp.sum(spec_im * band_re - spec_re * band_im, axis=0)
    frame_power = frame_power.reshape(stripes, count_frames, columns)
    partial = jnp.concatenate(
        [
            cross_re.reshape(stripes, count_frames * steps, columns),
            cross_im.reshape(stripes, count_frames * steps, columns),
            frame_power,
            jnp.broadcast_to(band_power[None], (stripes, steps, columns)),
        ],
        axis=1,
    )
    partial, received = lax.optimization_barrier((partial, received))
    total = jnp.sum(
        lax.all_to_all(partial, "stripe", split_axis=0, concat_axis=0, tiled=True), axis=0
    )
    pairs = count_frames * steps
    cross_re = total[:pairs].reshape(count_frames, steps, columns)
    cross_im = total[pairs : 2 * pairs].reshape(count_frames, steps, columns)
    frame_power = total[2 * pairs : 2 * pairs + count_frames]
    band_power = total[2 * pairs + count_frames :]

    magnitude = jnp.sqrt(frame_power[:, None, :] * band_power[None, :, :] + 1e-06)
    coh_re = (cross_re / magnitude).astype(jnp.bfloat16).astype(jnp.float32) * weight
    coh_im = (cross_im / magnitude).astype(jnp.bfloat16).astype(jnp.float32) * weight
    zeros = jnp.zeros_like(coh_re)
    coherence = jnp.concatenate(
        [
            jnp.concatenate([coh_re, zeros], axis=2),
            jnp.concatenate([zeros, coh_im], axis=2),
        ],
        axis=0,
    ).astype(jnp.bfloat16)
    parts = lax.dot_general(
        coherence.reshape(2 * count_frames * steps, 2 * columns),
        forward[:columns],
        (((1,), (1,)), ((), ())),
        preferred_element_type=jnp.float32,
    )
    even = parts[: count_frames * steps]
    odd = parts[count_frames * steps :]
    surface = jnp.concatenate(
        [(even + odd)[:, : half + 1], lax.rev((even - odd)[:, 1:half], (1,))], axis=1
    )
    correlation = (surface * math.sqrt(band_rows / pixels)).reshape(count_frames, steps, pixels)

    incoming = received[:, :, :pixels]
    index_f = received[:, :, pixels].astype(jnp.float32)
    hits = index_f[None, :, :] == jnp.arange(band_rows, dtype=jnp.float32)[:, None, None]
    landed = jnp.einsum(
        "tps,psx->tx", hits.astype(jnp.bfloat16), incoming, preferred_element_type=jnp.float32
    )
    land_count = jnp.sum(hits.astype(jnp.float32), axis=(1, 2))
    blended = (reference_img.astype(jnp.float32) + landed) / (1.0 + land_count[:, None])
    return (correlation, blended)


def solution(mesh):
    placed = (
        P(("stripe", "frame"), None),
        P(("stripe", "frame"), None, None),
        P(("stripe", "frame")),
        P(("stripe", "frame"), None),
        P(("stripe", "frame")),
        P(),
    )
    return jax.shard_map(
        per_device,
        mesh=mesh,
        in_specs=placed,
        out_specs=(P(("stripe", "frame"), None, None), P(("stripe", "frame"), None)),
        check_vma=False,
    )
```

```python
import math

import jax
import jax.numpy as jnp
from jax import lax
from jax.sharding import PartitionSpec as P


def dft_table(rows, columns, pixels):
    lo_count = 64 if rows % 64 == 0 else 1
    hi_count = rows // lo_count
    c = jnp.arange(columns, dtype=jnp.int32)
    scale = 2.0 * math.pi / pixels
    hi = jnp.arange(hi_count, dtype=jnp.int32)
    lo = jnp.arange(lo_count, dtype=jnp.int32)
    phase_hi = (hi[:, None] * lo_count * c[None, :] % pixels).astype(jnp.float32) * scale
    phase_lo = (lo[:, None] * c[None, :] % pixels).astype(jnp.float32) * scale
    c1, s1 = jnp.cos(phase_hi)[:, None, :], jnp.sin(phase_hi)[:, None, :]
    c2, s2 = jnp.cos(phase_lo)[None, :, :], jnp.sin(phase_lo)[None, :, :]
    cos_t = (c1 * c2 - s1 * s2).reshape(rows, columns)
    nsin_t = (-(s1 * c2 + c1 * s2)).reshape(rows, columns)
    return cos_t.astype(jnp.bfloat16), nsin_t.astype(jnp.bfloat16)


def shift_rows(frame_img, amount):
    pixels = frame_img.shape[-1]
    doubled = jnp.concatenate([frame_img, frame_img], axis=1)
    start = pixels - lax.rem(amount, pixels)
    return lax.dynamic_slice_in_dim(doubled, start, pixels, axis=1)


def per_device(reference_img, frames, shifts, dest_device, dest_row, visit_order):
    count_frames, band_rows, pixels = frames.shape
    steps = visit_order.shape[0]
    stripes = lax.axis_size("stripe")
    half = pixels // 2
    columns = min(pixels, half + 128)
    fwd_cos, fwd_sin = dft_table(pixels, columns, pixels)
    forward = jnp.concatenate([fwd_cos, fwd_sin], axis=1)
    col = jnp.arange(columns, dtype=jnp.int32)
    weight = jnp.where((col == 0) | (col == half), 1.0, jnp.where(col < half, 2.0, 0.0))

    chunk = band_rows // stripes
    outbound = jnp.concatenate(
        [frames[f].reshape(stripes, chunk, pixels) for f in range(count_frames)]
        + [reference_img.reshape(stripes, chunk, pixels)],
        axis=1,
    )
    inbound = lax.all_to_all(outbound, "stripe", split_axis=0, concat_axis=0, tiled=True)
    num_devices = lax.axis_size("stripe") * lax.axis_size("frame")
    frame_rows = count_frames * band_rows
    capacity = max(2, 2 * frame_rows // num_devices)
    placed = jnp.concatenate(
        [shift_rows(frames[f], shifts[f]) for f in range(count_frames)], axis=0
    )
    target_dev = dest_device[:, 0]
    onehot = (target_dev[:, None] == jnp.arange(num_devices, dtype=jnp.int32)[None, :]).astype(
        jnp.int32
    )
    row_rank = jnp.sum((jnp.cumsum(onehot, axis=0) - 1) * onehot, axis=1)
    slot_id = target_dev * capacity + row_rank
    select = slot_id[None, :] == jnp.arange(num_devices * capacity, dtype=jnp.int32)[:, None]
    select3 = select.reshape(num_devices, capacity, frame_rows)
    outgoing = jnp.einsum(
        "dsr,rx->dsx", select3.astype(jnp.bfloat16), placed, preferred_element_type=jnp.float32
    ).astype(jnp.bfloat16)
    filled = jnp.any(select3, axis=2)
    local_row = jnp.sum(jnp.where(select3, dest_row[None, None, :], 0), axis=2)
    out_index = jnp.where(filled, local_row, -1).astype(jnp.float32).astype(jnp.bfloat16)
    lanes = 128
    index_cols = jnp.broadcast_to(out_index[:, :, None], (num_devices, capacity, lanes))
    packed = jnp.concatenate([outgoing, index_cols], axis=2)
    received = lax.all_to_all(packed, ("stripe", "frame"), split_axis=0, concat_axis=0, tiled=True)
    frame_rows_in = (
        inbound[:, : count_frames * chunk]
        .reshape(stripes, count_frames, chunk, pixels)
        .transpose(2, 0, 1, 3)
        .reshape(chunk * stripes * count_frames, pixels)
    )
    band_in = inbound[:, count_frames * chunk :]
    visited = jnp.take(band_in, visit_order, axis=0, mode="clip").transpose(1, 0, 2)
    visited = visited.reshape(chunk * steps, pixels)

    spectra = jnp.dot(frame_rows_in, forward, preferred_element_type=jnp.float32).reshape(
        chunk, stripes * count_frames, 1, 2 * columns
    )
    spec_re = spectra[..., :columns]
    spec_im = spectra[..., columns:]
    band = (
        jnp.dot(visited, forward, preferred_element_type=jnp.float32)
        .astype(jnp.bfloat16)
        .astype(jnp.float32)
        .reshape(chunk, 1, steps, 2 * columns)
    )
    band_re = band[..., :columns]
    band_im = band[..., columns:]
    frame_power = jnp.sum(spec_re * spec_re + spec_im * spec_im, axis=0)[:, 0]
    band_power = jnp.sum(band_re * band_re + band_im * band_im, axis=0)[0]
    cross_re = jnp.sum(spec_re * band_re + spec_im * band_im, axis=0)
    cross_im = jnp.sum(spec_im * band_re - spec_re * band_im, axis=0)
    frame_power = frame_power.reshape(stripes, count_frames, columns)
    partial = jnp.concatenate(
        [
            cross_re.reshape(stripes, count_frames * steps, columns),
            cross_im.reshape(stripes, count_frames * steps, columns),
            frame_power,
            jnp.broadcast_to(band_power[None], (stripes, steps, columns)),
        ],
        axis=1,
    )
    partial, received = lax.optimization_barrier((partial, received))
    total = jnp.sum(
        lax.all_to_all(partial, "stripe", split_axis=0, concat_axis=0, tiled=True), axis=0
    )
    pairs = count_frames * steps
    cross_re = total[:pairs].reshape(count_frames, steps, columns)
    cross_im = total[pairs : 2 * pairs].reshape(count_frames, steps, columns)
    frame_power = total[2 * pairs : 2 * pairs + count_frames]
    band_power = total[2 * pairs + count_frames :]

    magnitude = jnp.sqrt(frame_power[:, None, :] * band_power[None, :, :] + 1e-06)
    coh_re = (cross_re / magnitude).astype(jnp.bfloat16).astype(jnp.float32) * weight
    coh_im = (cross_im / magnitude).astype(jnp.bfloat16).astype(jnp.float32) * weight
    coherence = jnp.concatenate([coh_re, coh_im], axis=2).astype(jnp.bfloat16)
    surface = lax.dot_general(
        coherence.reshape(count_frames * steps, 2 * columns),
        forward,
        (((1,), (1,)), ((), ())),
        preferred_element_type=jnp.float32,
    )
    correlation = (surface * math.sqrt(band_rows / pixels)).reshape(count_frames, steps, pixels)

    incoming = received[:, :, :pixels]
    index_f = received[:, :, pixels].astype(jnp.float32)
    hits = index_f[None, :, :] == jnp.arange(band_rows, dtype=jnp.float32)[:, None, None]
    landed = jnp.einsum(
        "tps,psx->tx", hits.astype(jnp.bfloat16), incoming, preferred_element_type=jnp.float32
    )
    land_count = jnp.sum(hits.astype(jnp.float32), axis=(1, 2))
    blended = (reference_img.astype(jnp.float32) + landed) / (1.0 + land_count[:, None])
    return (correlation, blended)


def solution(mesh):
    placed = (
        P(("stripe", "frame"), None),
        P(("stripe", "frame"), None, None),
        P(("stripe", "frame")),
        P(("stripe", "frame"), None),
        P(("stripe", "frame")),
        P(),
    )
    return jax.shard_map(
        per_device,
        mesh=mesh,
        in_specs=placed,
        out_specs=(P(("stripe", "frame"), None, None), P(("stripe", "frame"), None)),
        check_vma=False,
    )
```

```python
import math

import jax
import jax.numpy as jnp
from jax import lax
from jax.sharding import PartitionSpec as P


def dft_table(rows, columns, pixels):
    lo_count = 64 if rows % 64 == 0 else 1
    hi_count = rows // lo_count
    c = jnp.arange(columns, dtype=jnp.int32)
    scale = 2.0 * math.pi / pixels
    hi = jnp.arange(hi_count, dtype=jnp.int32)
    lo = jnp.arange(lo_count, dtype=jnp.int32)
    phase_hi = (hi[:, None] * lo_count * c[None, :] % pixels).astype(jnp.float32) * scale
    phase_lo = (lo[:, None] * c[None, :] % pixels).astype(jnp.float32) * scale
    c1, s1 = jnp.cos(phase_hi)[:, None, :], jnp.sin(phase_hi)[:, None, :]
    c2, s2 = jnp.cos(phase_lo)[None, :, :], jnp.sin(phase_lo)[None, :, :]
    cos_t = (c1 * c2 - s1 * s2).reshape(rows, columns)
    nsin_t = (-(s1 * c2 + c1 * s2)).reshape(rows, columns)
    return cos_t.astype(jnp.bfloat16), nsin_t.astype(jnp.bfloat16)


def shift_rows(frame_img, amount):
    pixels = frame_img.shape[-1]
    doubled = jnp.concatenate([frame_img, frame_img], axis=1)
    start = pixels - lax.rem(amount, pixels)
    return lax.dynamic_slice_in_dim(doubled, start, pixels, axis=1)


def per_device(reference_img, frames, shifts, dest_device, dest_row, visit_order):
    count_frames, band_rows, pixels = frames.shape
    steps = visit_order.shape[0]
    stripes = lax.axis_size("stripe")
    half = pixels // 2
    columns = min(pixels, half + 128)
    fwd_cos, fwd_sin = dft_table(pixels, columns, pixels)
    forward = jnp.concatenate([fwd_cos, fwd_sin], axis=1)
    col = jnp.arange(columns, dtype=jnp.int32)
    weight = jnp.where((col == 0) | (col == half), 1.0, jnp.where(col < half, 2.0, 0.0))

    chunk = band_rows // stripes
    outbound = jnp.concatenate(
        [frames[f].reshape(stripes, chunk, pixels) for f in range(count_frames)]
        + [reference_img.reshape(stripes, chunk, pixels)],
        axis=1,
    )
    inbound = lax.all_to_all(outbound, "stripe", split_axis=0, concat_axis=0, tiled=True)
    num_devices = lax.axis_size("stripe") * lax.axis_size("frame")
    frame_rows = count_frames * band_rows
    capacity = max(2, 2 * frame_rows // num_devices)
    placed = jnp.concatenate(
        [shift_rows(frames[f], shifts[f]) for f in range(count_frames)], axis=0
    )
    target_dev = dest_device[:, 0]
    onehot = (target_dev[:, None] == jnp.arange(num_devices, dtype=jnp.int32)[None, :]).astype(
        jnp.int32
    )
    row_rank = jnp.sum((jnp.cumsum(onehot, axis=0) - 1) * onehot, axis=1)
    slot_id = target_dev * capacity + row_rank
    select = slot_id[None, :] == jnp.arange(num_devices * capacity, dtype=jnp.int32)[:, None]
    select3 = select.reshape(num_devices, capacity, frame_rows)
    outgoing = jnp.einsum(
        "dsr,rx->dsx", select3.astype(jnp.bfloat16), placed, preferred_element_type=jnp.float32
    ).astype(jnp.bfloat16)
    filled = jnp.any(select3, axis=2)
    local_row = jnp.sum(jnp.where(select3, dest_row[None, None, :], 0), axis=2)
    out_index = jnp.where(filled, local_row, -1).astype(jnp.float32).astype(jnp.bfloat16)
    lanes = 128
    index_cols = jnp.broadcast_to(out_index[:, :, None], (num_devices, capacity, lanes))
    packed = jnp.concatenate([outgoing, index_cols], axis=2)
    received = lax.all_to_all(packed, ("stripe", "frame"), split_axis=0, concat_axis=0, tiled=True)
    frame_rows_in = (
        inbound[:, : count_frames * chunk]
        .reshape(stripes, count_frames, chunk, pixels)
        .transpose(2, 0, 1, 3)
        .reshape(chunk * stripes * count_frames, pixels)
    )
    band_in = inbound[:, count_frames * chunk :]
    visited = jnp.take(band_in, visit_order, axis=0, mode="clip").transpose(1, 0, 2)
    visited = visited.reshape(chunk * steps, pixels)

    spectra = jnp.dot(frame_rows_in, forward, preferred_element_type=jnp.float32).reshape(
        chunk, stripes * count_frames, 1, 2 * columns
    )
    spec_re = spectra[..., :columns]
    spec_im = spectra[..., columns:]
    band = (
        jnp.dot(visited, forward, preferred_element_type=jnp.float32)
        .astype(jnp.bfloat16)
        .astype(jnp.float32)
        .reshape(chunk, 1, steps, 2 * columns)
    )
    band_re = band[..., :columns]
    band_im = band[..., columns:]
    frame_power = jnp.sum(spec_re * spec_re + spec_im * spec_im, axis=0)[:, 0]
    band_power = jnp.sum(band_re * band_re + band_im * band_im, axis=0)[0]
    cross_re = jnp.sum(spec_re * band_re + spec_im * band_im, axis=0)
    cross_im = jnp.sum(spec_im * band_re - spec_re * band_im, axis=0)
    frame_power = frame_power.reshape(stripes, count_frames, columns)
    partial = jnp.concatenate(
        [
            cross_re.reshape(stripes, count_frames * steps, columns),
            cross_im.reshape(stripes, count_frames * steps, columns),
            frame_power,
            jnp.broadcast_to(band_power[None], (stripes, steps, columns)),
        ],
        axis=1,
    )
    partial, received = lax.optimization_barrier((partial, received))
    shares = lax.all_to_all(
        partial.astype(jnp.bfloat16), "stripe", split_axis=0, concat_axis=0, tiled=True
    )
    total = jnp.sum(shares.astype(jnp.float32), axis=0)
    pairs = count_frames * steps
    cross_re = total[:pairs].reshape(count_frames, steps, columns)
    cross_im = total[pairs : 2 * pairs].reshape(count_frames, steps, columns)
    frame_power = total[2 * pairs : 2 * pairs + count_frames]
    band_power = total[2 * pairs + count_frames :]

    magnitude = jnp.sqrt(frame_power[:, None, :] * band_power[None, :, :] + 1e-06)
    coh_re = (cross_re / magnitude).astype(jnp.bfloat16).astype(jnp.float32) * weight
    coh_im = (cross_im / magnitude).astype(jnp.bfloat16).astype(jnp.float32) * weight
    coherence = jnp.concatenate([coh_re, coh_im], axis=2).astype(jnp.bfloat16)
    surface = lax.dot_general(
        coherence.reshape(count_frames * steps, 2 * columns),
        forward,
        (((1,), (1,)), ((), ())),
        preferred_element_type=jnp.float32,
    )
    correlation = (surface * math.sqrt(band_rows / pixels)).reshape(count_frames, steps, pixels)

    incoming = received[:, :, :pixels]
    index_f = received[:, :, pixels].astype(jnp.float32)
    hits = index_f[None, :, :] == jnp.arange(band_rows, dtype=jnp.float32)[:, None, None]
    landed = jnp.einsum(
        "tps,psx->tx", hits.astype(jnp.bfloat16), incoming, preferred_element_type=jnp.float32
    )
    land_count = jnp.sum(hits.astype(jnp.float32), axis=(1, 2))
    blended = (reference_img.astype(jnp.float32) + landed) / (1.0 + land_count[:, None])
    return (correlation, blended)


def solution(mesh):
    placed = (
        P(("stripe", "frame"), None),
        P(("stripe", "frame"), None, None),
        P(("stripe", "frame")),
        P(("stripe", "frame"), None),
        P(("stripe", "frame")),
        P(),
    )
    return jax.shard_map(
        per_device,
        mesh=mesh,
        in_specs=placed,
        out_specs=(P(("stripe", "frame"), None, None), P(("stripe", "frame"), None)),
        check_vma=False,
    )
```

```python
import math

import jax
import jax.numpy as jnp
from jax import lax
from jax.sharding import PartitionSpec as P


def dft_table(rows, columns, pixels):
    lo_count = 64 if rows % 64 == 0 else 1
    hi_count = rows // lo_count
    c = jnp.arange(columns, dtype=jnp.int32)
    scale = 2.0 * math.pi / pixels
    hi = jnp.arange(hi_count, dtype=jnp.int32)
    lo = jnp.arange(lo_count, dtype=jnp.int32)
    phase_hi = (hi[:, None] * lo_count * c[None, :] % pixels).astype(jnp.float32) * scale
    phase_lo = (lo[:, None] * c[None, :] % pixels).astype(jnp.float32) * scale
    c1, s1 = jnp.cos(phase_hi)[:, None, :], jnp.sin(phase_hi)[:, None, :]
    c2, s2 = jnp.cos(phase_lo)[None, :, :], jnp.sin(phase_lo)[None, :, :]
    cos_t = (c1 * c2 - s1 * s2).reshape(rows, columns)
    nsin_t = (-(s1 * c2 + c1 * s2)).reshape(rows, columns)
    return cos_t.astype(jnp.bfloat16), nsin_t.astype(jnp.bfloat16)


def shift_rows(frame_img, amount):
    pixels = frame_img.shape[-1]
    doubled = jnp.concatenate([frame_img, frame_img], axis=1)
    start = pixels - lax.rem(amount, pixels)
    return lax.dynamic_slice_in_dim(doubled, start, pixels, axis=1)


def per_device(reference_img, frames, shifts, dest_device, dest_row, visit_order):
    count_frames, band_rows, pixels = frames.shape
    steps = visit_order.shape[0]
    stripes = lax.axis_size("stripe")
    half = pixels // 2
    columns = min(pixels, half + 128)
    fwd_cos, fwd_sin = dft_table(pixels, columns, pixels)
    forward = jnp.concatenate([fwd_cos, fwd_sin], axis=1)
    col = jnp.arange(columns, dtype=jnp.int32)
    weight = jnp.where((col == 0) | (col == half), 1.0, jnp.where(col < half, 2.0, 0.0))

    chunk = band_rows // stripes
    outbound = jnp.concatenate(
        [frames[f].reshape(stripes, chunk, pixels) for f in range(count_frames)]
        + [reference_img.reshape(stripes, chunk, pixels)],
        axis=1,
    )
    inbound = lax.all_to_all(outbound, "stripe", split_axis=0, concat_axis=0, tiled=True)
    num_devices = lax.axis_size("stripe") * lax.axis_size("frame")
    frame_rows = count_frames * band_rows
    capacity = max(2, 2 * frame_rows // num_devices)
    placed = jnp.concatenate(
        [shift_rows(frames[f], shifts[f]) for f in range(count_frames)], axis=0
    )
    target_dev = dest_device[:, 0]
    onehot = (target_dev[:, None] == jnp.arange(num_devices, dtype=jnp.int32)[None, :]).astype(
        jnp.int32
    )
    row_rank = jnp.sum((jnp.cumsum(onehot, axis=0) - 1) * onehot, axis=1)
    slot_id = target_dev * capacity + row_rank
    select = slot_id[None, :] == jnp.arange(num_devices * capacity, dtype=jnp.int32)[:, None]
    select3 = select.reshape(num_devices, capacity, frame_rows)
    outgoing = jnp.einsum(
        "dsr,rx->dsx", select3.astype(jnp.bfloat16), placed, preferred_element_type=jnp.float32
    ).astype(jnp.bfloat16)
    filled = jnp.any(select3, axis=2)
    local_row = jnp.sum(jnp.where(select3, dest_row[None, None, :], 0), axis=2)
    out_index = jnp.where(filled, local_row, -1).astype(jnp.float32).astype(jnp.bfloat16)
    lanes = 128
    index_cols = jnp.broadcast_to(out_index[:, :, None], (num_devices, capacity, lanes))
    packed = jnp.concatenate([outgoing, index_cols], axis=2)
    received = lax.all_to_all(packed, ("stripe", "frame"), split_axis=0, concat_axis=0, tiled=True)
    frame_rows_in = (
        inbound[:, : count_frames * chunk]
        .reshape(stripes, count_frames, chunk, pixels)
        .transpose(2, 0, 1, 3)
        .reshape(chunk * stripes * count_frames, pixels)
    )
    band_in = inbound[:, count_frames * chunk :]
    visited = jnp.take(band_in, visit_order, axis=0, mode="clip").transpose(1, 0, 2)
    visited = visited.reshape(chunk * steps, pixels)

    spectra = jnp.dot(frame_rows_in, forward, preferred_element_type=jnp.float32).reshape(
        chunk, stripes * count_frames, 1, 2 * columns
    )
    spec_re = spectra[..., :columns]
    spec_im = spectra[..., columns:]
    band = (
        jnp.dot(visited, forward, preferred_element_type=jnp.float32)
        .astype(jnp.bfloat16)
        .astype(jnp.float32)
        .reshape(chunk, 1, steps, 2 * columns)
    )
    band_re = band[..., :columns]
    band_im = band[..., columns:]
    frame_power = jnp.sum(spec_re * spec_re + spec_im * spec_im, axis=0)[:, 0]
    band_power = jnp.sum(band_re * band_re + band_im * band_im, axis=0)[0]
    cross_re = jnp.sum(spec_re * band_re + spec_im * band_im, axis=0)
    cross_im = jnp.sum(spec_im * band_re - spec_re * band_im, axis=0)
    frame_power = frame_power.reshape(stripes, count_frames, columns)
    partial = jnp.concatenate(
        [
            cross_re.reshape(stripes, count_frames * steps, columns),
            cross_im.reshape(stripes, count_frames * steps, columns),
            frame_power,
            jnp.broadcast_to(band_power[None], (stripes, steps, columns)),
        ],
        axis=1,
    )
    partial, received = lax.optimization_barrier((partial, received))
    rows = partial.shape[1]
    nyquist = jnp.pad(partial[:, :, half], ((0, 0), (0, half - rows)))[:, None, :]
    outgoing_sums = jnp.concatenate([partial[:, :, :half], nyquist], axis=1)
    shares = lax.all_to_all(
        outgoing_sums.astype(jnp.bfloat16), "stripe", split_axis=0, concat_axis=0, tiled=True
    )
    summed = jnp.sum(shares.astype(jnp.float32), axis=0)
    total = jnp.concatenate(
        [
            summed[:rows],
            summed[rows, :rows, None],
            jnp.zeros((rows, columns - half - 1), jnp.float32),
        ],
        axis=1,
    )
    pairs = count_frames * steps
    cross_re = total[:pairs].reshape(count_frames, steps, columns)
    cross_im = total[pairs : 2 * pairs].reshape(count_frames, steps, columns)
    frame_power = total[2 * pairs : 2 * pairs + count_frames]
    band_power = total[2 * pairs + count_frames :]

    magnitude = jnp.sqrt(frame_power[:, None, :] * band_power[None, :, :] + 1e-06)
    coh_re = (cross_re / magnitude).astype(jnp.bfloat16).astype(jnp.float32) * weight
    coh_im = (cross_im / magnitude).astype(jnp.bfloat16).astype(jnp.float32) * weight
    coherence = jnp.concatenate([coh_re, coh_im], axis=2).astype(jnp.bfloat16)
    surface = lax.dot_general(
        coherence.reshape(count_frames * steps, 2 * columns),
        forward,
        (((1,), (1,)), ((), ())),
        preferred_element_type=jnp.float32,
    )
    correlation = (surface * math.sqrt(band_rows / pixels)).reshape(count_frames, steps, pixels)

    incoming = received[:, :, :pixels]
    index_f = received[:, :, pixels].astype(jnp.float32)
    hits = index_f[None, :, :] == jnp.arange(band_rows, dtype=jnp.float32)[:, None, None]
    landed = jnp.einsum(
        "tps,psx->tx", hits.astype(jnp.bfloat16), incoming, preferred_element_type=jnp.float32
    )
    land_count = jnp.sum(hits.astype(jnp.float32), axis=(1, 2))
    blended = (reference_img.astype(jnp.float32) + landed) / (1.0 + land_count[:, None])
    return (correlation, blended)


def solution(mesh):
    placed = (
        P(("stripe", "frame"), None),
        P(("stripe", "frame"), None, None),
        P(("stripe", "frame")),
        P(("stripe", "frame"), None),
        P(("stripe", "frame")),
        P(),
    )
    return jax.shard_map(
        per_device,
        mesh=mesh,
        in_specs=placed,
        out_specs=(P(("stripe", "frame"), None, None), P(("stripe", "frame"), None)),
        check_vma=False,
    )
```

```python
import math

import jax
import jax.numpy as jnp
from jax import lax
from jax.sharding import PartitionSpec as P


def dft_table(rows, columns, pixels):
    lo_count = 64 if rows % 64 == 0 else 1
    hi_count = rows // lo_count
    c = jnp.arange(columns, dtype=jnp.int32)
    scale = 2.0 * math.pi / pixels
    hi = jnp.arange(hi_count, dtype=jnp.int32)
    lo = jnp.arange(lo_count, dtype=jnp.int32)
    phase_hi = (hi[:, None] * lo_count * c[None, :] % pixels).astype(jnp.float32) * scale
    phase_lo = (lo[:, None] * c[None, :] % pixels).astype(jnp.float32) * scale
    c1, s1 = jnp.cos(phase_hi)[:, None, :], jnp.sin(phase_hi)[:, None, :]
    c2, s2 = jnp.cos(phase_lo)[None, :, :], jnp.sin(phase_lo)[None, :, :]
    cos_t = (c1 * c2 - s1 * s2).reshape(rows, columns)
    nsin_t = (-(s1 * c2 + c1 * s2)).reshape(rows, columns)
    return cos_t.astype(jnp.bfloat16), nsin_t.astype(jnp.bfloat16)


def shift_rows(frame_img, amount):
    pixels = frame_img.shape[-1]
    doubled = jnp.concatenate([frame_img, frame_img], axis=1)
    start = pixels - lax.rem(amount, pixels)
    return lax.dynamic_slice_in_dim(doubled, start, pixels, axis=1)


def per_device(reference_img, frames, shifts, dest_device, dest_row, visit_order):
    count_frames, band_rows, pixels = frames.shape
    steps = visit_order.shape[0]
    stripes = lax.axis_size("stripe")
    half = pixels // 2
    columns = min(pixels, half + 128)
    fwd_cos, fwd_sin = dft_table(pixels, columns, pixels)
    forward = jnp.concatenate([fwd_cos, fwd_sin], axis=1)
    col = jnp.arange(columns, dtype=jnp.int32)
    weight = jnp.where((col == 0) | (col == half), 1.0, jnp.where(col < half, 2.0, 0.0))

    chunk = band_rows // stripes
    outbound = jnp.concatenate(
        [frames[f].reshape(stripes, chunk, pixels) for f in range(count_frames)]
        + [reference_img.reshape(stripes, chunk, pixels)],
        axis=1,
    )
    inbound = lax.all_to_all(outbound, "stripe", split_axis=0, concat_axis=0, tiled=True)
    num_devices = lax.axis_size("stripe") * lax.axis_size("frame")
    frame_rows = count_frames * band_rows
    capacity = max(2, 2 * frame_rows // num_devices)
    placed = jnp.concatenate(
        [shift_rows(frames[f], shifts[f]) for f in range(count_frames)], axis=0
    )
    target_dev = dest_device[:, 0]
    onehot = (target_dev[:, None] == jnp.arange(num_devices, dtype=jnp.int32)[None, :]).astype(
        jnp.int32
    )
    row_rank = jnp.sum((jnp.cumsum(onehot, axis=0) - 1) * onehot, axis=1)
    slot_id = target_dev * capacity + row_rank
    select = slot_id[None, :] == jnp.arange(num_devices * capacity, dtype=jnp.int32)[:, None]
    select3 = select.reshape(num_devices, capacity, frame_rows)
    outgoing = jnp.einsum(
        "dsr,rx->dsx", select3.astype(jnp.bfloat16), placed, preferred_element_type=jnp.float32
    ).astype(jnp.bfloat16)
    filled = jnp.any(select3, axis=2)
    local_row = jnp.sum(jnp.where(select3, dest_row[None, None, :], 0), axis=2)
    out_index = jnp.where(filled, local_row, -1).astype(jnp.float32).astype(jnp.bfloat16)
    lanes = 128
    index_cols = jnp.broadcast_to(out_index[:, :, None], (num_devices, capacity, lanes))
    packed = jnp.concatenate([outgoing, index_cols], axis=2)
    received = lax.all_to_all(packed, ("stripe", "frame"), split_axis=0, concat_axis=0, tiled=True)
    frame_rows_in = (
        inbound[:, : count_frames * chunk]
        .reshape(stripes, count_frames, chunk, pixels)
        .transpose(2, 0, 1, 3)
        .reshape(chunk * stripes * count_frames, pixels)
    )
    band_in = inbound[:, count_frames * chunk :]
    visited = jnp.take(band_in, visit_order, axis=0, mode="clip").transpose(1, 0, 2)
    visited = visited.reshape(chunk * steps, pixels)

    spectra = jnp.dot(frame_rows_in, forward, preferred_element_type=jnp.float32).reshape(
        chunk, stripes * count_frames, 1, 2 * columns
    )
    spec_re = spectra[..., :columns]
    spec_im = spectra[..., columns:]
    band = (
        jnp.dot(visited, forward, preferred_element_type=jnp.float32)
        .astype(jnp.bfloat16)
        .astype(jnp.float32)
        .reshape(chunk, 1, steps, 2 * columns)
    )
    band_re = band[..., :columns]
    band_im = band[..., columns:]
    frame_power = jnp.sum(spec_re * spec_re + spec_im * spec_im, axis=0)[:, 0]
    band_power = jnp.sum(band_re * band_re + band_im * band_im, axis=0)[0]
    cross_re = jnp.sum(spec_re * band_re + spec_im * band_im, axis=0)
    cross_im = jnp.sum(spec_im * band_re - spec_re * band_im, axis=0)
    frame_power = frame_power.reshape(stripes, count_frames, columns)
    partial = jnp.concatenate(
        [
            cross_re.reshape(stripes, count_frames * steps, columns),
            cross_im.reshape(stripes, count_frames * steps, columns),
            frame_power,
            jnp.broadcast_to(band_power[None], (stripes, steps, columns)),
        ],
        axis=1,
    )
    partial, received = lax.optimization_barrier((partial, received))
    shares = lax.all_to_all(
        partial.astype(jnp.bfloat16), "stripe", split_axis=0, concat_axis=0, tiled=True
    )
    total = jnp.sum(shares.astype(jnp.float32), axis=0)
    pairs = count_frames * steps
    cross_re = total[:pairs].reshape(count_frames, steps, columns)
    cross_im = total[pairs : 2 * pairs].reshape(count_frames, steps, columns)
    frame_power = total[2 * pairs : 2 * pairs + count_frames]
    band_power = total[2 * pairs + count_frames :]

    magnitude = jnp.sqrt(frame_power[:, None, :] * band_power[None, :, :] + 1e-06)
    coh_re = (cross_re / magnitude).astype(jnp.bfloat16).astype(jnp.float32) * weight
    coh_im = (cross_im / magnitude).astype(jnp.bfloat16).astype(jnp.float32) * weight
    zeros = jnp.zeros_like(coh_re)
    coherence = jnp.concatenate(
        [
            jnp.concatenate([coh_re, zeros], axis=2),
            jnp.concatenate([zeros, coh_im], axis=2),
        ],
        axis=0,
    ).astype(jnp.bfloat16)
    parts = lax.dot_general(
        coherence.reshape(2 * count_frames * steps, 2 * columns),
        forward[:columns],
        (((1,), (1,)), ((), ())),
        preferred_element_type=jnp.float32,
    )
    even = parts[: count_frames * steps]
    odd = parts[count_frames * steps :]
    surface = jnp.concatenate(
        [(even + odd)[:, : half + 1], lax.rev((even - odd)[:, 1:half], (1,))], axis=1
    )
    correlation = (surface * math.sqrt(band_rows / pixels)).reshape(count_frames, steps, pixels)

    incoming = received[:, :, :pixels]
    index_f = received[:, :, pixels].astype(jnp.float32)
    hits = index_f[None, :, :] == jnp.arange(band_rows, dtype=jnp.float32)[:, None, None]
    landed = jnp.einsum(
        "tps,psx->tx", hits.astype(jnp.bfloat16), incoming, preferred_element_type=jnp.float32
    )
    land_count = jnp.sum(hits.astype(jnp.float32), axis=(1, 2))
    blended = (reference_img.astype(jnp.float32) + landed) / (1.0 + land_count[:, None])
    return (correlation, blended)


def solution(mesh):
    placed = (
        P(("stripe", "frame"), None),
        P(("stripe", "frame"), None, None),
        P(("stripe", "frame")),
        P(("stripe", "frame"), None),
        P(("stripe", "frame")),
        P(),
    )
    return jax.shard_map(
        per_device,
        mesh=mesh,
        in_specs=placed,
        out_specs=(P(("stripe", "frame"), None, None), P(("stripe", "frame"), None)),
        check_vma=False,
    )
```
